32 devices in a mesh: space: 4 (over z), vel: 8 (over y, x, core).
Axes of the slice: x: 2, y: 2, z: 4, core: 2. Of those that a mesh axis runs over, the one named last changes fastest.
Arguments:
- distribution: bfloat16 [4096, 24, 8, 128], P('vel', 'space'), may hold values from -6 to 6
- up_factor: bfloat16 [4096, 256], P('vel'), may hold values from -0.75 to 0.75
- down_factor: bfloat16 [4096, 256], P('vel'), may hold values from -0.09375 to 0.09375
- decay: float32 [4096], P('vel'), may hold values from 0.3 to 3
- wall_kind: int32 [2, 8, 128], replicated, may hold values from 0 to 2
Outputs:
- advanced: bfloat16 [4096, 24, 8, 128], P('vel', 'space')
The draws below stay inside these ranges and needn't reach their ends.
Inputs may be any that keep to these rules, and one draw needn't show every extreme that they name: `wall_kind`: 0 marks a diffuse wall at rest, 1 a diffuse heated wall, 2 an open face.
All inputs are finite; a program needn't handle non-finite values.
Results may differ from the reference program's by a relative error of at most 0.0046.
Values may be sent and summed in bfloat16 or wider, within the bound.
No kernel may reach another device: no remote copies, remote signals or barrier semaphores. Data moves between devices by JAX's collectives and lax.ppermute only.
A program may use at most 192 MiB of HBM per device.

```python
import math
import jax
import jax.numpy as jnp
from jax import lax

NV = 16
R = 256
V = 4096
GX = 8
GY = 128
STEPS = 2
NZ = 24


def place_ends(array, rng, least, top_value):
    longest = array.shape.index(max(array.shape))
    spots = []
    for shift in (0, 1):
        where = [jax.random.randint(jax.random.fold_in(rng, axis), (), 0, length) for axis, length in enumerate(array.shape)]
        where[longest] = (where[longest] + shift) % array.shape[longest]
        spots.append(tuple(where))
    return array.at[spots[0]].set(least).at[spots[1]].set(top_value)


def block_levels(stream_key, dims, cuts, low, high):
    gain = 1.0
    for axis_at, blocks in cuts:
        draws = jax.random.uniform(jax.random.fold_in(jax.random.fold_in(stream_key, 6), axis_at), (blocks,), jnp.float32, low / len(cuts), high / len(cuts))
        gain = gain * jnp.repeat(jnp.exp(draws), dims[axis_at] // blocks).reshape((-1,) + (1,) * (len(dims) - 1 - axis_at))
    return gain


def scatter_about(stream_key, extent, spread, most, pieces=(), kind=jnp.bfloat16):
    level = block_levels(stream_key, extent, pieces, -0.22, 0.18) if pieces else 1.0
    drawn = jax.random.normal(stream_key, extent, jnp.float32) * spread * level
    return jnp.minimum(jnp.maximum(drawn, -most), most).astype(kind)


def setup_inputs(seed: int = 0) -> dict:
    streams_of = jax.random.split(jax.random.key(seed), 6)
    distribution = scatter_about(streams_of[0], (V, NZ, GX, GY), 1.0, 6.0, ((0, 8), (1, 4)))
    up_factor = scatter_about(streams_of[1], (V, R), (R // 4) ** -0.5, 0.75, ((0, 8),))
    down_factor = scatter_about(streams_of[2], (V, R), V ** -0.5, 0.09375, ((0, 8),))
    decay = jnp.clip(jnp.exp(math.log(3.0) - 2.3025851 * jax.random.uniform(streams_of[3], (V,), jnp.float32) ** block_levels(streams_of[3], (V,), ((0, 8),), -0.2, 0.2)), 0.3, 3.0)
    wall_kind = place_ends(jax.random.randint(streams_of[4], (2, GX, GY), 0, 3), jax.random.fold_in(streams_of[4], 1), 0, 2).astype(jnp.int32)
    return {"distribution": distribution, "up_factor": up_factor, "down_factor": down_factor, "decay": decay, "wall_kind": wall_kind}


speed_range = 8.0
time_ratio = 0.08
wall_heat = 3.0


def components(vel_ids):
    spacing = speed_range / NV
    midpoint = (NV - 1) / 2.0
    along_z = ((vel_ids // (NV * NV)).astype(jnp.float32) - midpoint) * spacing
    along_x = (((vel_ids // NV) % NV).astype(jnp.float32) - midpoint) * spacing
    along_y = ((vel_ids % NV).astype(jnp.float32) - midpoint) * spacing
    return along_z, along_x, along_y


def wall_ghost(outflux, kind_face, maxwell, energy, norm):
    sigma = outflux / norm
    heating = jnp.where(kind_face == 1, wall_heat, 0.0)
    opened = jnp.where(kind_face == 2, 0.0, 1.0)
    return maxwell[:, None, None] * (sigma[None] + heating[None] * energy[:, None, None]) * opened[None]


def transport(centre, lower_plane, upper_plane, along_z, along_x, along_y):
    dimensions = centre.ndim
    shaped = (-1,) + (1,) * (dimensions - 1)
    axis_x = dimensions - 2
    axis_y = dimensions - 1
    plus_z = jnp.maximum(along_z, 0.0).reshape(shaped)
    minus_z = jnp.minimum(along_z, 0.0).reshape(shaped)
    plus_x = jnp.maximum(along_x, 0.0).reshape(shaped)
    minus_x = jnp.minimum(along_x, 0.0).reshape(shaped)
    plus_y = jnp.maximum(along_y, 0.0).reshape(shaped)
    minus_y = jnp.minimum(along_y, 0.0).reshape(shaped)
    result = plus_z * (centre - lower_plane) + minus_z * (upper_plane - centre)
    result = result + plus_x * (centre - jnp.roll(centre, 1, axis_x)) + minus_x * (jnp.roll(centre, -1, axis_x) - centre)
    result = result + plus_y * (centre - jnp.roll(centre, 1, axis_y)) + minus_y * (jnp.roll(centre, -1, axis_y) - centre)
    return result


def advance(current, up_factor, down_factor, decay, wall_kind, along_z, along_x, along_y, maxwell, energy, norm):
    depth = current.shape[1]
    low_face = current[:, 0].astype(jnp.float32)
    high_face = current[:, depth - 1].astype(jnp.float32)
    outflux_low = jnp.sum(jnp.maximum(-along_z, 0.0)[:, None, None] * low_face, axis=0)
    outflux_high = jnp.sum(jnp.maximum(along_z, 0.0)[:, None, None] * high_face, axis=0)
    ghost_low = wall_ghost(outflux_low, wall_kind[0], maxwell, energy, norm)
    ghost_high = wall_ghost(outflux_high, wall_kind[1], maxwell, energy, norm)

    def plane(level):
        stored = lax.dynamic_index_in_dim(current, level, 1, keepdims=False)
        centre = stored.astype(jnp.float32)
        lower_raw = lax.dynamic_index_in_dim(current, jnp.maximum(level - 1, 0), 1, keepdims=False)
        upper_raw = lax.dynamic_index_in_dim(current, jnp.minimum(level + 1, depth - 1), 1, keepdims=False)
        lower_plane = jnp.where(level == 0, ghost_low, lower_raw.astype(jnp.float32))
        upper_plane = jnp.where(level == depth - 1, ghost_high, upper_raw.astype(jnp.float32))
        moved = transport(centre, lower_plane, upper_plane, along_z, along_x, along_y)
        flat_rows = stored.reshape(stored.shape[0], -1)
        coeffs = jnp.dot(down_factor.T, flat_rows, preferred_element_type=jnp.float32).astype(jnp.bfloat16)
        gained = jnp.dot(up_factor, coeffs, preferred_element_type=jnp.float32).reshape(centre.shape)
        updated = centre - time_ratio * moved + time_ratio * (gained - decay[:, None, None] * centre)
        return updated.astype(jnp.bfloat16)

    planes = lax.map(plane, jnp.arange(depth, dtype=jnp.int32))
    return jnp.transpose(planes, (1, 0, 2, 3))


def reference(distribution, up_factor, down_factor, decay, wall_kind):
    all_ids = jnp.arange(NV ** 3, dtype=jnp.int32)
    along_z, along_x, along_y = components(all_ids)
    speed_sq = along_z * along_z + along_x * along_x + along_y * along_y
    maxwell = jnp.exp(-0.5 * speed_sq)
    energy = 0.5 * speed_sq - 1.5
    norm = jnp.sum(jnp.maximum(along_z, 0.0) * maxwell)
    current = distribution
    for step in range(STEPS):
        current = advance(current, up_factor, down_factor, decay, wall_kind, along_z, along_x, along_y, maxwell, energy, norm)
    return current
```

```python
import functools

import jax
import jax.numpy as jnp
from jax import lax
from jax.experimental import pallas as pl
from jax.experimental.pallas import tpu as pltpu
from jax.sharding import PartitionSpec as P

NV = 16
STEPS = 2


speed_range = 8.0
time_ratio = 0.08
wall_heat = 3.0


def components(vel_ids):
    spacing = speed_range / NV
    midpoint = (NV - 1) / 2.0
    along_z = ((vel_ids // (NV * NV)).astype(jnp.float32) - midpoint) * spacing
    along_x = ((vel_ids // NV % NV).astype(jnp.float32) - midpoint) * spacing
    along_y = ((vel_ids % NV).astype(jnp.float32) - midpoint) * spacing
    return (along_z, along_x, along_y)


def wall_ghost(outflux, kind_face, maxwell, energy, norm):
    sigma = outflux / norm
    heating = jnp.where(kind_face == 1, wall_heat, 0.0)
    opened = jnp.where(kind_face == 2, 0.0, 1.0)
    return (
        maxwell[:, None]
        * (sigma[None] + heating[None] * energy[:, None])
        * opened[None]
    )


def update_kernel(par_ref, up_ref, coef_ref, cur_ref, lo_ref, hi_ref, out_ref, work_ref, *, depth, plane, width):
    work_ref[:, 0:plane] = lo_ref[...]
    work_ref[:, (depth + 1) * plane:(depth + 2) * plane] = hi_ref[...]
    work_ref[:, plane:(depth + 1) * plane] = cur_ref[...].astype(jnp.float32)
    rows = plane // width
    up = up_ref[...]

    def one_plane(z, carry):
        base = pl.multiple_of((z + 1) * plane, plane)
        gained = jnp.dot(
            up, coef_ref[:, pl.ds(pl.multiple_of(z * plane, plane), plane)],
            preferred_element_type=jnp.float32,
        )
        for x in range(rows):
            at = base + x * width
            xm = base + ((x - 1) % rows) * width
            xp = base + ((x + 1) % rows) * width
            c = work_ref[:, pl.ds(at, width)]
            lo = work_ref[:, pl.ds(at - plane, width)]
            hi = work_ref[:, pl.ds(at + plane, width)]
            left = work_ref[:, pl.ds(xm, width)]
            right = work_ref[:, pl.ds(xp, width)]
            down_y = pltpu.roll(c, 1, 1)
            up_y = pltpu.roll(c, width - 1, 1)
            total = (
                par_ref[0] * c
                + par_ref[1] * lo
                + par_ref[2] * hi
                + par_ref[3] * left
                + par_ref[4] * right
                + par_ref[5] * down_y
                + par_ref[6] * up_y
                + time_ratio * gained[:, x * width:(x + 1) * width]
            )
            out_ref[:, pl.ds(pl.multiple_of(z * plane + x * width, width), width)] = total.astype(out_ref.dtype)
        return carry

    lax.fori_loop(0, depth, one_plane, 0)


def body(distribution, up_factor, down_factor, decay, wall_kind):
    local_vel, depth, width_x, width_y = distribution.shape
    plane = width_x * width_y
    cells = depth * plane
    rank = up_factor.shape[1]
    vel_ids = lax.axis_index("vel") * local_vel + jnp.arange(local_vel, dtype=jnp.int32)
    along_z, along_x, along_y = components(vel_ids)
    speed_sq = along_z * along_z + along_x * along_x + along_y * along_y
    maxwell = jnp.exp(-0.5 * speed_sq)
    energy = 0.5 * speed_sq - 1.5
    all_ids = jnp.arange(NV**3, dtype=jnp.int32)
    full_z, full_x, full_y = components(all_ids)
    norm = jnp.sum(
        jnp.maximum(full_z, 0.0)
        * jnp.exp(-0.5 * (full_z * full_z + full_x * full_x + full_y * full_y))
    )
    slab = lax.axis_index("space")
    slabs = lax.axis_size("space")
    dt = time_ratio
    per_vel = jnp.stack(
        [
            1.0 - dt * (jnp.abs(along_z) + jnp.abs(along_x) + jnp.abs(along_y)) - dt * decay,
            dt * jnp.maximum(along_z, 0.0),
            -dt * jnp.minimum(along_z, 0.0),
            dt * jnp.maximum(along_x, 0.0),
            -dt * jnp.minimum(along_x, 0.0),
            dt * jnp.maximum(along_y, 0.0),
            -dt * jnp.minimum(along_y, 0.0),
        ]
    )
    params = jnp.broadcast_to(per_vel[:, :, None], (7, local_vel, width_y))
    wl = jnp.maximum(-along_z, 0.0)
    wh = jnp.maximum(along_z, 0.0)
    count = slabs
    forward = [(i, i + 1) for i in range(count - 1)]
    backward = [(i + 1, i) for i in range(count - 1)]

    vb = 128
    kernel = functools.partial(update_kernel, depth=depth, plane=plane, width=width_y)
    update = pl.pallas_call(
        kernel,
        grid=(local_vel // vb,),
        in_specs=[
            pl.BlockSpec((7, vb, width_y), lambda i: (0, i, 0)),
            pl.BlockSpec((vb, rank), lambda i: (i, 0)),
            pl.BlockSpec((rank, cells), lambda i: (0, 0)),
            pl.BlockSpec((vb, cells), lambda i: (i, 0)),
            pl.BlockSpec((vb, plane), lambda i: (i, 0)),
            pl.BlockSpec((vb, plane), lambda i: (i, 0)),
        ],
        out_specs=pl.BlockSpec((vb, cells), lambda i: (i, 0)),
        out_shape=jax.ShapeDtypeStruct((local_vel, cells), jnp.bfloat16),
        scratch_shapes=[pltpu.VMEM((vb, cells + 2 * plane), jnp.float32)],
        compiler_params=pltpu.CompilerParams(vmem_limit_bytes=48 * 1024 * 1024),
    )

    current = distribution.reshape(local_vel, cells)
    for step in range(STEPS):
        low_face = current[:, :plane]
        high_face = current[:, cells - plane:]
        out_low = jnp.sum(wl[:, None] * low_face.astype(jnp.float32), axis=0)
        out_high = jnp.sum(wh[:, None] * high_face.astype(jnp.float32), axis=0)
        outflux = lax.psum(jnp.stack([out_low, out_high]), "vel")
        ghost_low = wall_ghost(outflux[0], wall_kind[0].reshape(plane), maxwell, energy, norm)
        ghost_high = wall_ghost(outflux[1], wall_kind[1].reshape(plane), maxwell, energy, norm)
        from_below = lax.ppermute(high_face, "space", forward)
        from_above = lax.ppermute(low_face, "space", backward)
        lower_plane = jnp.where(slab == 0, ghost_low, from_below.astype(jnp.float32))
        upper_plane = jnp.where(slab == slabs - 1, ghost_high, from_above.astype(jnp.float32))
        partial = lax.dot_general(
            down_factor, current, (((0,), (0,)), ((), ())), preferred_element_type=jnp.float32
        )
        coeffs = lax.psum_scatter(partial, "vel", scatter_dimension=1, tiled=True).astype(jnp.bfloat16)
        coeffs = lax.all_gather(coeffs, "vel", axis=1, tiled=True)
        current = update(params, up_factor, coeffs, current, lower_plane, upper_plane)
    return current.reshape(local_vel, depth, width_x, width_y)


def solution(mesh):
    return jax.shard_map(
        body,
        mesh=mesh,
        in_specs=(P("vel", "space", None, None), P("vel", None), P("vel", None), P("vel"), P()),
        out_specs=P("vel", "space", None, None),
        check_vma=False,
    )
```

```python
import functools

import jax
import jax.numpy as jnp
from jax import lax
from jax.experimental import pallas as pl
from jax.experimental.pallas import tpu as pltpu
from jax.sharding import PartitionSpec as P

NV = 16
STEPS = 2


speed_range = 8.0
time_ratio = 0.08
wall_heat = 3.0


def components(vel_ids):
    spacing = speed_range / NV
    midpoint = (NV - 1) / 2.0
    along_z = ((vel_ids // (NV * NV)).astype(jnp.float32) - midpoint) * spacing
    along_x = ((vel_ids // NV % NV).astype(jnp.float32) - midpoint) * spacing
    along_y = ((vel_ids % NV).astype(jnp.float32) - midpoint) * spacing
    return (along_z, along_x, along_y)


def wall_ghost(outflux, kind_face, maxwell, energy, norm):
    sigma = outflux / norm
    heating = jnp.where(kind_face == 1, wall_heat, 0.0)
    opened = jnp.where(kind_face == 2, 0.0, 1.0)
    return (
        maxwell[:, None]
        * (sigma[None] + heating[None] * energy[:, None])
        * opened[None]
    )


def update_kernel(par_ref, up_ref, coef_ref, cur_ref, lo_ref, hi_ref, out_ref, work_ref, *, depth, plane, width):
    work_ref[:, 0:plane] = lo_ref[...]
    work_ref[:, (depth + 1) * plane:(depth + 2) * plane] = hi_ref[...]
    work_ref[:, plane:(depth + 1) * plane] = cur_ref[...].astype(jnp.float32)
    rows = plane // width
    up = up_ref[...]

    def one_plane(z, carry):
        base = pl.multiple_of((z + 1) * plane, plane)
        gained = jnp.dot(
            up, coef_ref[:, pl.ds(pl.multiple_of(z * plane, plane), plane)],
            preferred_element_type=jnp.float32,
        )
        for x in range(rows):
            at = base + x * width
            xm = base + ((x - 1) % rows) * width
            xp = base + ((x + 1) % rows) * width
            c = work_ref[:, pl.ds(at, width)]
            lo = work_ref[:, pl.ds(at - plane, width)]
            hi = work_ref[:, pl.ds(at + plane, width)]
            left = work_ref[:, pl.ds(xm, width)]
            right = work_ref[:, pl.ds(xp, width)]
            down_y = pltpu.roll(c, 1, 1)
            up_y = pltpu.roll(c, width - 1, 1)
            total = (
                par_ref[0] * c
                + par_ref[1] * lo
                + par_ref[2] * hi
                + par_ref[3] * left
                + par_ref[4] * right
                + par_ref[5] * down_y
                + par_ref[6] * up_y
                + time_ratio * gained[:, x * width:(x + 1) * width]
            )
            out_ref[:, pl.ds(pl.multiple_of(z * plane + x * width, width), width)] = total.astype(out_ref.dtype)
        return carry

    lax.fori_loop(0, depth, one_plane, 0)


def body(distribution, up_factor, down_factor, decay, wall_kind):
    local_vel, depth, width_x, width_y = distribution.shape
    plane = width_x * width_y
    cells = depth * plane
    rank = up_factor.shape[1]
    vel_ids = lax.axis_index("vel") * local_vel + jnp.arange(local_vel, dtype=jnp.int32)
    along_z, along_x, along_y = components(vel_ids)
    speed_sq = along_z * along_z + along_x * along_x + along_y * along_y
    maxwell = jnp.exp(-0.5 * speed_sq)
    energy = 0.5 * speed_sq - 1.5
    all_ids = jnp.arange(NV**3, dtype=jnp.int32)
    full_z, full_x, full_y = components(all_ids)
    norm = jnp.sum(
        jnp.maximum(full_z, 0.0)
        * jnp.exp(-0.5 * (full_z * full_z + full_x * full_x + full_y * full_y))
    )
    slab = lax.axis_index("space")
    slabs = lax.axis_size("space")
    dt = time_ratio
    per_vel = jnp.stack(
        [
            1.0 - dt * (jnp.abs(along_z) + jnp.abs(along_x) + jnp.abs(along_y)) - dt * decay,
            dt * jnp.maximum(along_z, 0.0),
            -dt * jnp.minimum(along_z, 0.0),
            dt * jnp.maximum(along_x, 0.0),
            -dt * jnp.minimum(along_x, 0.0),
            dt * jnp.maximum(along_y, 0.0),
            -dt * jnp.minimum(along_y, 0.0),
        ]
    )
    params = jnp.broadcast_to(per_vel[:, :, None], (7, local_vel, width_y))
    wl = jnp.maximum(-along_z, 0.0)
    wh = jnp.maximum(along_z, 0.0)
    count = slabs
    forward = [(i, i + 1) for i in range(count - 1)]
    backward = [(i + 1, i) for i in range(count - 1)]

    vb = 128
    kernel = functools.partial(update_kernel, depth=depth, plane=plane, width=width_y)
    update = pl.pallas_call(
        kernel,
        grid=(local_vel // vb,),
        in_specs=[
            pl.BlockSpec((7, vb, width_y), lambda i: (0, i, 0)),
            pl.BlockSpec((vb, rank), lambda i: (i, 0)),
            pl.BlockSpec((rank, cells), lambda i: (0, 0)),
            pl.BlockSpec((vb, cells), lambda i: (i, 0)),
            pl.BlockSpec((vb, plane), lambda i: (i, 0)),
            pl.BlockSpec((vb, plane), lambda i: (i, 0)),
        ],
        out_specs=pl.BlockSpec((vb, cells), lambda i: (i, 0)),
        out_shape=jax.ShapeDtypeStruct((local_vel, cells), jnp.bfloat16),
        scratch_shapes=[pltpu.VMEM((vb, cells + 2 * plane), jnp.float32)],
        compiler_params=pltpu.CompilerParams(vmem_limit_bytes=48 * 1024 * 1024),
    )

    current = distribution.reshape(local_vel, cells)
    for step in range(STEPS):
        low_face = current[:, :plane]
        high_face = current[:, cells - plane:]
        out_low = jnp.sum(wl[:, None] * low_face.astype(jnp.float32), axis=0)
        out_high = jnp.sum(wh[:, None] * high_face.astype(jnp.float32), axis=0)
        outflux = jnp.sum(lax.all_gather(jnp.stack([out_low, out_high]), "vel"), axis=0)
        ghost_low = wall_ghost(outflux[0], wall_kind[0].reshape(plane), maxwell, energy, norm)
        ghost_high = wall_ghost(outflux[1], wall_kind[1].reshape(plane), maxwell, energy, norm)
        from_below = lax.ppermute(high_face, "space", forward)
        from_above = lax.ppermute(low_face, "space", backward)
        lower_plane = jnp.where(slab == 0, ghost_low, from_below.astype(jnp.float32))
        upper_plane = jnp.where(slab == slabs - 1, ghost_high, from_above.astype(jnp.float32))
        partial = lax.dot_general(
            down_factor, current, (((0,), (0,)), ((), ())), preferred_element_type=jnp.float32
        ).astype(jnp.bfloat16)
        coeffs = lax.psum_scatter(partial, "vel", scatter_dimension=0, tiled=True)
        coeffs = lax.all_gather(coeffs, "vel", axis=0, tiled=True)
        current = update(params, up_factor, coeffs, current, lower_plane, upper_plane)
    return current.reshape(local_vel, depth, width_x, width_y)


def solution(mesh):
    return jax.shard_map(
        body,
        mesh=mesh,
        in_specs=(P("vel", "space", None, None), P("vel", None), P("vel", None), P("vel"), P()),
        out_specs=P("vel", "space", None, None),
        check_vma=False,
    )
```

```python
import functools

import jax
import jax.numpy as jnp
from jax import lax
from jax.experimental import pallas as pl
from jax.experimental.pallas import tpu as pltpu
from jax.sharding import PartitionSpec as P


NV = 16
STEPS = 2


speed_range = 8.0
time_ratio = 0.08
wall_heat = 3.0


def components(vel_ids):
    spacing = speed_range / NV
    midpoint = (NV - 1) / 2.0
    along_z = ((vel_ids // (NV * NV)).astype(jnp.float32) - midpoint) * spacing
    along_x = ((vel_ids // NV % NV).astype(jnp.float32) - midpoint) * spacing
    along_y = ((vel_ids % NV).astype(jnp.float32) - midpoint) * spacing
    return (along_z, along_x, along_y)


def wall_ghost(outflux, kind_face, maxwell, energy, norm):
    sigma = outflux / norm
    heating = jnp.where(kind_face == 1, wall_heat, 0.0)
    opened = jnp.where(kind_face == 2, 0.0, 1.0)
    return (
        maxwell[:, None]
        * (sigma[None] + heating[None] * energy[:, None])
        * opened[None]
    )


def transport_kernel(par_ref, cur_ref, lo_ref, hi_ref, out_ref, work_ref, *, depth, plane, width):
    work_ref[:, 0:plane] = lo_ref[...]
    work_ref[:, (depth + 1) * plane:(depth + 2) * plane] = hi_ref[...]
    work_ref[:, plane:(depth + 1) * plane] = cur_ref[...].astype(jnp.float32)
    rows = plane // width

    def one_plane(z, carry):
        base = pl.multiple_of((z + 1) * plane, plane)
        for x in range(rows):
            at = base + x * width
            xm = base + ((x - 1) % rows) * width
            xp = base + ((x + 1) % rows) * width
            c = work_ref[:, pl.ds(at, width)]
            lo = work_ref[:, pl.ds(at - plane, width)]
            hi = work_ref[:, pl.ds(at + plane, width)]
            left = work_ref[:, pl.ds(xm, width)]
            right = work_ref[:, pl.ds(xp, width)]
            down_y = pltpu.roll(c, 1, 1)
            up_y = pltpu.roll(c, width - 1, 1)
            total = (
                par_ref[0] * c
                + par_ref[1] * lo
                + par_ref[2] * hi
                + par_ref[3] * left
                + par_ref[4] * right
                + par_ref[5] * down_y
                + par_ref[6] * up_y
            )
            out_ref[:, pl.ds(pl.multiple_of(z * plane + x * width, width), width)] = total
        return carry

    lax.fori_loop(0, depth, one_plane, 0)


def collide_kernel(up_ref, coef_ref, base_ref, out_ref, *, depth, plane):
    up = up_ref[...]

    def one_plane(z, carry):
        at = pl.multiple_of(z * plane, plane)
        gained = lax.dot_general(
            up, coef_ref[pl.ds(at, plane), :], (((1,), (1,)), ((), ())),
            preferred_element_type=jnp.float32,
        )
        out_ref[:, pl.ds(at, plane)] = (base_ref[:, pl.ds(at, plane)] + time_ratio * gained).astype(out_ref.dtype)
        return carry

    lax.fori_loop(0, depth, one_plane, 0)


def vel_sum(value):
    count = lax.axis_size("vel")
    hop = 1
    while hop < count:
        value = value + lax.ppermute(value, "vel", [(i, i ^ hop) for i in range(count)])
        hop *= 2
    return value


def body(distribution, up_factor, down_factor, decay, wall_kind):
    local_vel, depth, width_x, width_y = distribution.shape
    plane = width_x * width_y
    cells = depth * plane
    rank = up_factor.shape[1]
    vel_ids = lax.axis_index("vel") * local_vel + jnp.arange(local_vel, dtype=jnp.int32)
    along_z, along_x, along_y = components(vel_ids)
    speed_sq = along_z * along_z + along_x * along_x + along_y * along_y
    maxwell = jnp.exp(-0.5 * speed_sq)
    energy = 0.5 * speed_sq - 1.5
    all_ids = jnp.arange(NV**3, dtype=jnp.int32)
    full_z, full_x, full_y = components(all_ids)
    norm = jnp.sum(
        jnp.maximum(full_z, 0.0)
        * jnp.exp(-0.5 * (full_z * full_z + full_x * full_x + full_y * full_y))
    )
    slab = lax.axis_index("space")
    slabs = lax.axis_size("space")
    dt = time_ratio
    per_vel = jnp.stack(
        [
            1.0 - dt * (jnp.abs(along_z) + jnp.abs(along_x) + jnp.abs(along_y)) - dt * decay,
            dt * jnp.maximum(along_z, 0.0),
            -dt * jnp.minimum(along_z, 0.0),
            dt * jnp.maximum(along_x, 0.0),
            -dt * jnp.minimum(along_x, 0.0),
            dt * jnp.maximum(along_y, 0.0),
            -dt * jnp.minimum(along_y, 0.0),
        ]
    )
    params = jnp.broadcast_to(per_vel[:, :, None], (7, local_vel, width_y))
    wl = jnp.maximum(-along_z, 0.0)
    wh = jnp.maximum(along_z, 0.0)
    count = slabs
    forward = [(i, i + 1) for i in range(count - 1)]
    backward = [(i + 1, i) for i in range(count - 1)]

    vb = 128
    transport = pl.pallas_call(
        functools.partial(transport_kernel, depth=depth, plane=plane, width=width_y),
        grid=(local_vel // vb,),
        in_specs=[
            pl.BlockSpec((7, vb, width_y), lambda i: (0, i, 0)),
            pl.BlockSpec((vb, cells), lambda i: (i, 0)),
            pl.BlockSpec((vb, plane), lambda i: (i, 0)),
            pl.BlockSpec((vb, plane), lambda i: (i, 0)),
        ],
        out_specs=pl.BlockSpec((vb, cells), lambda i: (i, 0)),
        out_shape=jax.ShapeDtypeStruct((local_vel, cells), jnp.float32),
        scratch_shapes=[pltpu.VMEM((vb, cells + 2 * plane), jnp.float32)],
        compiler_params=pltpu.CompilerParams(vmem_limit_bytes=48 * 1024 * 1024),
    )
    collide = pl.pallas_call(
        functools.partial(collide_kernel, depth=depth, plane=plane),
        grid=(local_vel // vb,),
        in_specs=[
            pl.BlockSpec((vb, rank), lambda i: (i, 0)),
            pl.BlockSpec((cells, rank), lambda i: (0, 0)),
            pl.BlockSpec((vb, cells), lambda i: (i, 0)),
        ],
        out_specs=pl.BlockSpec((vb, cells), lambda i: (i, 0)),
        out_shape=jax.ShapeDtypeStruct((local_vel, cells), jnp.bfloat16),
        compiler_params=pltpu.CompilerParams(vmem_limit_bytes=48 * 1024 * 1024),
    )

    current = distribution.reshape(local_vel, cells)
    for step in range(STEPS):
        low_face = current[:, :plane]
        high_face = current[:, cells - plane:]
        out_low = jnp.sum(wl[:, None] * low_face.astype(jnp.float32), axis=0)
        out_high = jnp.sum(wh[:, None] * high_face.astype(jnp.float32), axis=0)
        outflux = vel_sum(jnp.stack([out_low, out_high]))
        ghost_low = wall_ghost(outflux[0], wall_kind[0].reshape(plane), maxwell, energy, norm)
        ghost_high = wall_ghost(outflux[1], wall_kind[1].reshape(plane), maxwell, energy, norm)
        from_below = lax.ppermute(high_face, "space", forward)
        from_above = lax.ppermute(low_face, "space", backward)
        lower_plane = jnp.where(slab == 0, ghost_low, from_below.astype(jnp.float32))
        upper_plane = jnp.where(slab == slabs - 1, ghost_high, from_above.astype(jnp.float32))
        partial = lax.dot_general(
            current, down_factor, (((0,), (0,)), ((), ())), preferred_element_type=jnp.float32
        )
        coeffs = lax.psum_scatter(partial, "vel", scatter_dimension=0, tiled=True)
        base = transport(params, current, lower_plane, upper_plane)
        coeffs, base = lax.optimization_barrier((coeffs, base))
        coeffs = lax.all_gather(coeffs.astype(jnp.bfloat16), "vel", axis=0, tiled=True)
        current = collide(up_factor, coeffs, base)
    return current.reshape(local_vel, depth, width_x, width_y)


def solution(mesh):
    return jax.shard_map(
        body,
        mesh=mesh,
        in_specs=(P("vel", "space", None, None), P("vel", None), P("vel", None), P("vel"), P()),
        out_specs=P("vel", "space", None, None),
        check_vma=False,
    )
```

```python
import functools

import jax
import jax.numpy as jnp
from jax import lax
from jax.experimental import pallas as pl
from jax.experimental.pallas import tpu as pltpu
from jax.sharding import PartitionSpec as P


NV = 16
STEPS = 2


speed_range = 8.0
time_ratio = 0.08
wall_heat = 3.0


def components(vel_ids):
    spacing = speed_range / NV
    midpoint = (NV - 1) / 2.0
    along_z = ((vel_ids // (NV * NV)).astype(jnp.float32) - midpoint) * spacing
    along_x = ((vel_ids // NV % NV).astype(jnp.float32) - midpoint) * spacing
    along_y = ((vel_ids % NV).astype(jnp.float32) - midpoint) * spacing
    return (along_z, along_x, along_y)


def wall_ghost(outflux, kind_face, maxwell, energy, norm):
    sigma = outflux / norm
    heating = jnp.where(kind_face == 1, wall_heat, 0.0)
    opened = jnp.where(kind_face == 2, 0.0, 1.0)
    return (
        maxwell[:, None]
        * (sigma[None] + heating[None] * energy[:, None])
        * opened[None]
    )


def transport_kernel(par_ref, cur_ref, lo_ref, hi_ref, out_ref, work_ref, *, depth, plane, width):
    work_ref[:, 0:plane] = lo_ref[...]
    work_ref[:, (depth + 1) * plane:(depth + 2) * plane] = hi_ref[...]
    work_ref[:, plane:(depth + 1) * plane] = cur_ref[...].astype(jnp.float32)
    rows = plane // width

    def one_plane(z, carry):
        base = pl.multiple_of((z + 1) * plane, plane)
        for x in range(rows):
            at = base + x * width
            xm = base + ((x - 1) % rows) * width
            xp = base + ((x + 1) % rows) * width
            c = work_ref[:, pl.ds(at, width)]
            lo = work_ref[:, pl.ds(at - plane, width)]
            hi = work_ref[:, pl.ds(at + plane, width)]
            left = work_ref[:, pl.ds(xm, width)]
            right = work_ref[:, pl.ds(xp, width)]
            down_y = pltpu.roll(c, 1, 1)
            up_y = pltpu.roll(c, width - 1, 1)
            total = (
                par_ref[0] * c
                + par_ref[1] * lo
                + par_ref[2] * hi
                + par_ref[3] * left
                + par_ref[4] * right
                + par_ref[5] * down_y
                + par_ref[6] * up_y
            )
            out_ref[:, pl.ds(pl.multiple_of(z * plane + x * width, width), width)] = total
        return carry

    lax.fori_loop(0, depth, one_plane, 0)


def collide_kernel(up_ref, coef_ref, base_ref, out_ref, *, depth, plane):
    up = up_ref[...]

    def one_plane(z, carry):
        at = pl.multiple_of(z * plane, plane)
        gained = lax.dot_general(
            up, coef_ref[pl.ds(at, plane), :], (((1,), (1,)), ((), ())),
            preferred_element_type=jnp.float32,
        )
        out_ref[:, pl.ds(at, plane)] = (base_ref[:, pl.ds(at, plane)] + time_ratio * gained).astype(out_ref.dtype)
        return carry

    lax.fori_loop(0, depth, one_plane, 0)


def vel_sum(value):
    count = lax.axis_size("vel")
    hop = 1
    while hop < count:
        value = value + lax.ppermute(value, "vel", [(i, i ^ hop) for i in range(count)])
        hop *= 2
    return value


def halves(value, bit):
    pair = value.reshape((2, value.shape[0] // 2) + value.shape[1:])
    return lax.dynamic_index_in_dim(pair, bit, 0, False), lax.dynamic_index_in_dim(pair, 1 - bit, 0, False)


def joined(mine, theirs, bit):
    return jnp.where(bit == 0, jnp.concatenate([mine, theirs]), jnp.concatenate([theirs, mine]))


def swap(value, hop):
    count = lax.axis_size("vel")
    return lax.ppermute(value, "vel", [(i, i ^ hop) for i in range(count)])


def vel_orders():
    count = lax.axis_size("vel")
    levels = count.bit_length() - 1
    return [1 << b for b in range(1, levels)], [1 << b for b in range(levels - 1, 0, -1)]


def reduce_scatter_rows(value):
    me = lax.axis_index("vel")
    keep, give = halves(value, me % 2)
    value = keep + swap(give, 1)
    first, second = halves(value, 0)
    order_a, order_b = vel_orders()
    for hop_a, hop_b in zip(order_a, order_b):
        keep_a, give_a = halves(first, (me // hop_a) % 2)
        keep_b, give_b = halves(second, (me // hop_b) % 2)
        first = keep_a + swap(give_a, hop_a)
        second = keep_b + swap(give_b, hop_b)
    return first, second


def all_gather_rows(first, second):
    me = lax.axis_index("vel")
    order_a, order_b = vel_orders()
    for hop_a, hop_b in zip(order_a[::-1], order_b[::-1]):
        first = joined(first, swap(first, hop_a), (me // hop_a) % 2)
        second = joined(second, swap(second, hop_b), (me // hop_b) % 2)
    value = jnp.concatenate([first, second])
    return joined(value, swap(value, 1), me % 2)


def body(distribution, up_factor, down_factor, decay, wall_kind):
    local_vel, depth, width_x, width_y = distribution.shape
    plane = width_x * width_y
    cells = depth * plane
    rank = up_factor.shape[1]
    vel_ids = lax.axis_index("vel") * local_vel + jnp.arange(local_vel, dtype=jnp.int32)
    along_z, along_x, along_y = components(vel_ids)
    speed_sq = along_z * along_z + along_x * along_x + along_y * along_y
    maxwell = jnp.exp(-0.5 * speed_sq)
    energy = 0.5 * speed_sq - 1.5
    all_ids = jnp.arange(NV**3, dtype=jnp.int32)
    full_z, full_x, full_y = components(all_ids)
    norm = jnp.sum(
        jnp.maximum(full_z, 0.0)
        * jnp.exp(-0.5 * (full_z * full_z + full_x * full_x + full_y * full_y))
    )
    slab = lax.axis_index("space")
    slabs = lax.axis_size("space")
    dt = time_ratio
    per_vel = jnp.stack(
        [
            1.0 - dt * (jnp.abs(along_z) + jnp.abs(along_x) + jnp.abs(along_y)) - dt * decay,
            dt * jnp.maximum(along_z, 0.0),
            -dt * jnp.minimum(along_z, 0.0),
            dt * jnp.maximum(along_x, 0.0),
            -dt * jnp.minimum(along_x, 0.0),
            dt * jnp.maximum(along_y, 0.0),
            -dt * jnp.minimum(along_y, 0.0),
        ]
    )
    params = jnp.broadcast_to(per_vel[:, :, None], (7, local_vel, width_y))
    wl = jnp.maximum(-along_z, 0.0)
    wh = jnp.maximum(along_z, 0.0)
    count = slabs
    forward = [(i, i + 1) for i in range(count - 1)]
    backward = [(i + 1, i) for i in range(count - 1)]

    vb = 128
    transport = pl.pallas_call(
        functools.partial(transport_kernel, depth=depth, plane=plane, width=width_y),
        grid=(local_vel // vb,),
        in_specs=[
            pl.BlockSpec((7, vb, width_y), lambda i: (0, i, 0)),
            pl.BlockSpec((vb, cells), lambda i: (i, 0)),
            pl.BlockSpec((vb, plane), lambda i: (i, 0)),
            pl.BlockSpec((vb, plane), lambda i: (i, 0)),
        ],
        out_specs=pl.BlockSpec((vb, cells), lambda i: (i, 0)),
        out_shape=jax.ShapeDtypeStruct((local_vel, cells), jnp.float32),
        scratch_shapes=[pltpu.VMEM((vb, cells + 2 * plane), jnp.float32)],
        compiler_params=pltpu.CompilerParams(vmem_limit_bytes=48 * 1024 * 1024),
    )
    collide = pl.pallas_call(
        functools.partial(collide_kernel, depth=depth, plane=plane),
        grid=(local_vel // vb,),
        in_specs=[
            pl.BlockSpec((vb, rank), lambda i: (i, 0)),
            pl.BlockSpec((cells, rank), lambda i: (0, 0)),
            pl.BlockSpec((vb, cells), lambda i: (i, 0)),
        ],
        out_specs=pl.BlockSpec((vb, cells), lambda i: (i, 0)),
        out_shape=jax.ShapeDtypeStruct((local_vel, cells), jnp.bfloat16),
        compiler_params=pltpu.CompilerParams(vmem_limit_bytes=48 * 1024 * 1024),
    )

    current = distribution.reshape(local_vel, cells)
    for step in range(STEPS):
        low_face = current[:, :plane]
        high_face = current[:, cells - plane:]
        out_low = jnp.sum(wl[:, None] * low_face.astype(jnp.float32), axis=0)
        out_high = jnp.sum(wh[:, None] * high_face.astype(jnp.float32), axis=0)
        outflux = vel_sum(jnp.stack([out_low, out_high]))
        ghost_low = wall_ghost(outflux[0], wall_kind[0].reshape(plane), maxwell, energy, norm)
        ghost_high = wall_ghost(outflux[1], wall_kind[1].reshape(plane), maxwell, energy, norm)
        from_below = lax.ppermute(high_face, "space", forward)
        from_above = lax.ppermute(low_face, "space", backward)
        lower_plane = jnp.where(slab == 0, ghost_low, from_below.astype(jnp.float32))
        upper_plane = jnp.where(slab == slabs - 1, ghost_high, from_above.astype(jnp.float32))
        partial = lax.dot_general(
            current, down_factor, (((0,), (0,)), ((), ())), preferred_element_type=jnp.float32
        )
        first, second = reduce_scatter_rows(partial)
        base = transport(params, current, lower_plane, upper_plane)
        coeffs = all_gather_rows(first.astype(jnp.bfloat16), second.astype(jnp.bfloat16))
        current = collide(up_factor, coeffs, base)
    return current.reshape(local_vel, depth, width_x, width_y)


def solution(mesh):
    return jax.shard_map(
        body,
        mesh=mesh,
        in_specs=(P("vel", "space", None, None), P("vel", None), P("vel", None), P("vel"), P()),
        out_specs=P("vel", "space", None, None),
        check_vma=False,
    )
```

```python
import functools

import jax
import jax.numpy as jnp
from jax import lax
from jax.experimental import pallas as pl
from jax.experimental.pallas import tpu as pltpu
from jax.sharding import PartitionSpec as P


NV = 16
STEPS = 2


speed_range = 8.0
time_ratio = 0.08
wall_heat = 3.0


def components(vel_ids):
    spacing = speed_range / NV
    midpoint = (NV - 1) / 2.0
    along_z = ((vel_ids // (NV * NV)).astype(jnp.float32) - midpoint) * spacing
    along_x = ((vel_ids // NV % NV).astype(jnp.float32) - midpoint) * spacing
    along_y = ((vel_ids % NV).astype(jnp.float32) - midpoint) * spacing
    return (along_z, along_x, along_y)


def wall_ghost(outflux, kind_face, maxwell, energy, norm):
    sigma = outflux / norm
    heating = jnp.where(kind_face == 1, wall_heat, 0.0)
    opened = jnp.where(kind_face == 2, 0.0, 1.0)
    return (
        maxwell[:, None]
        * (sigma[None] + heating[None] * energy[:, None])
        * opened[None]
    )


def transport_kernel(par_ref, cur_ref, lo_ref, hi_ref, out_ref, work_ref, *, depth, plane, width):
    work_ref[:, 0:plane] = lo_ref[...]
    work_ref[:, (depth + 1) * plane:(depth + 2) * plane] = hi_ref[...]
    work_ref[:, plane:(depth + 1) * plane] = cur_ref[...].astype(jnp.float32)
    rows = plane // width

    def one_plane(z, carry):
        base = pl.multiple_of((z + 1) * plane, plane)
        for x in range(rows):
            at = base + x * width
            xm = base + ((x - 1) % rows) * width
            xp = base + ((x + 1) % rows) * width
            c = work_ref[:, pl.ds(at, width)]
            lo = work_ref[:, pl.ds(at - plane, width)]
            hi = work_ref[:, pl.ds(at + plane, width)]
            left = work_ref[:, pl.ds(xm, width)]
            right = work_ref[:, pl.ds(xp, width)]
            down_y = pltpu.roll(c, 1, 1)
            up_y = pltpu.roll(c, width - 1, 1)
            total = (
                par_ref[0] * c
                + par_ref[1] * lo
                + par_ref[2] * hi
                + par_ref[3] * left
                + par_ref[4] * right
                + par_ref[5] * down_y
                + par_ref[6] * up_y
            )
            out_ref[:, pl.ds(pl.multiple_of(z * plane + x * width, width), width)] = total
        return carry

    lax.fori_loop(0, depth, one_plane, 0)


def collide_kernel(up_ref, coef_ref, base_ref, out_ref, *, depth, plane):
    up = up_ref[...]

    def one_plane(z, carry):
        at = pl.multiple_of(z * plane, plane)
        gained = lax.dot_general(
            up, coef_ref[pl.ds(at, plane), :], (((1,), (1,)), ((), ())),
            preferred_element_type=jnp.float32,
        )
        out_ref[:, pl.ds(at, plane)] = (base_ref[:, pl.ds(at, plane)] + time_ratio * gained).astype(out_ref.dtype)
        return carry

    lax.fori_loop(0, depth, one_plane, 0)


def vel_sum(value):
    count = lax.axis_size("vel")
    hop = 1
    while hop < count:
        value = value + lax.ppermute(value, "vel", [(i, i ^ hop) for i in range(count)])
        hop *= 2
    return value


def halves(value, bit):
    pair = value.reshape((2, value.shape[0] // 2) + value.shape[1:])
    return lax.dynamic_index_in_dim(pair, bit, 0, False), lax.dynamic_index_in_dim(pair, 1 - bit, 0, False)


def joined(mine, theirs, bit):
    return jnp.where(bit == 0, jnp.concatenate([mine, theirs]), jnp.concatenate([theirs, mine]))


def swap(value, hop):
    count = lax.axis_size("vel")
    return lax.ppermute(value, "vel", [(i, i ^ hop) for i in range(count)])


def vel_orders():
    count = lax.axis_size("vel")
    levels = count.bit_length() - 1
    return [1 << b for b in range(1, levels)], [1 << b for b in range(levels - 1, 0, -1)]


def reduce_scatter_rows(value, cover):
    me = lax.axis_index("vel")
    keep, give = halves(value, me % 2)
    value = keep + swap(give, 1)
    value, cover = lax.optimization_barrier((value, cover()))
    first, second = halves(value, 0)
    order_a, order_b = vel_orders()
    for hop_a, hop_b in zip(order_a, order_b):
        keep_a, give_a = halves(first, (me // hop_a) % 2)
        keep_b, give_b = halves(second, (me // hop_b) % 2)
        first = keep_a + swap(give_a, hop_a)
        second = keep_b + swap(give_b, hop_b)
    return first, second, cover


def all_gather_rows(first, second):
    me = lax.axis_index("vel")
    order_a, order_b = vel_orders()
    for hop_a, hop_b in zip(order_a[::-1], order_b[::-1]):
        first = joined(first, swap(first, hop_a), (me // hop_a) % 2)
        second = joined(second, swap(second, hop_b), (me // hop_b) % 2)
    value = jnp.concatenate([first, second])
    return joined(value, swap(value, 1), me % 2)


def body(distribution, up_factor, down_factor, decay, wall_kind):
    local_vel, depth, width_x, width_y = distribution.shape
    plane = width_x * width_y
    cells = depth * plane
    rank = up_factor.shape[1]
    vel_ids = lax.axis_index("vel") * local_vel + jnp.arange(local_vel, dtype=jnp.int32)
    along_z, along_x, along_y = components(vel_ids)
    speed_sq = along_z * along_z + along_x * along_x + along_y * along_y
    maxwell = jnp.exp(-0.5 * speed_sq)
    energy = 0.5 * speed_sq - 1.5
    all_ids = jnp.arange(NV**3, dtype=jnp.int32)
    full_z, full_x, full_y = components(all_ids)
    norm = jnp.sum(
        jnp.maximum(full_z, 0.0)
        * jnp.exp(-0.5 * (full_z * full_z + full_x * full_x + full_y * full_y))
    )
    slab = lax.axis_index("space")
    slabs = lax.axis_size("space")
    dt = time_ratio
    per_vel = jnp.stack(
        [
            1.0 - dt * (jnp.abs(along_z) + jnp.abs(along_x) + jnp.abs(along_y)) - dt * decay,
            dt * jnp.maximum(along_z, 0.0),
            -dt * jnp.minimum(along_z, 0.0),
            dt * jnp.maximum(along_x, 0.0),
            -dt * jnp.minimum(along_x, 0.0),
            dt * jnp.maximum(along_y, 0.0),
            -dt * jnp.minimum(along_y, 0.0),
        ]
    )
    params = jnp.broadcast_to(per_vel[:, :, None], (7, local_vel, width_y))
    wl = jnp.maximum(-along_z, 0.0)
    wh = jnp.maximum(along_z, 0.0)
    count = slabs
    forward = [(i, i + 1) for i in range(count - 1)]
    backward = [(i + 1, i) for i in range(count - 1)]

    vb = 128
    transport = pl.pallas_call(
        functools.partial(transport_kernel, depth=depth, plane=plane, width=width_y),
        grid=(local_vel // vb,),
        in_specs=[
            pl.BlockSpec((7, vb, width_y), lambda i: (0, i, 0)),
            pl.BlockSpec((vb, cells), lambda i: (i, 0)),
            pl.BlockSpec((vb, plane), lambda i: (i, 0)),
            pl.BlockSpec((vb, plane), lambda i: (i, 0)),
        ],
        out_specs=pl.BlockSpec((vb, cells), lambda i: (i, 0)),
        out_shape=jax.ShapeDtypeStruct((local_vel, cells), jnp.float32),
        scratch_shapes=[pltpu.VMEM((vb, cells + 2 * plane), jnp.float32)],
        compiler_params=pltpu.CompilerParams(vmem_limit_bytes=48 * 1024 * 1024),
    )
    collide = pl.pallas_call(
        functools.partial(collide_kernel, depth=depth, plane=plane),
        grid=(local_vel // vb,),
        in_specs=[
            pl.BlockSpec((vb, rank), lambda i: (i, 0)),
            pl.BlockSpec((cells, rank), lambda i: (0, 0)),
            pl.BlockSpec((vb, cells), lambda i: (i, 0)),
        ],
        out_specs=pl.BlockSpec((vb, cells), lambda i: (i, 0)),
        out_shape=jax.ShapeDtypeStruct((local_vel, cells), jnp.bfloat16),
        compiler_params=pltpu.CompilerParams(vmem_limit_bytes=48 * 1024 * 1024),
    )

    current = distribution.reshape(local_vel, cells)
    for step in range(STEPS):
        low_face = current[:, :plane]
        high_face = current[:, cells - plane:]
        out_low = jnp.sum(wl[:, None] * low_face.astype(jnp.float32), axis=0)
        out_high = jnp.sum(wh[:, None] * high_face.astype(jnp.float32), axis=0)
        outflux = vel_sum(jnp.stack([out_low, out_high]))
        ghost_low = wall_ghost(outflux[0], wall_kind[0].reshape(plane), maxwell, energy, norm)
        ghost_high = wall_ghost(outflux[1], wall_kind[1].reshape(plane), maxwell, energy, norm)
        from_below = lax.ppermute(high_face, "space", forward)
        from_above = lax.ppermute(low_face, "space", backward)
        lower_plane = jnp.where(slab == 0, ghost_low, from_below.astype(jnp.float32))
        upper_plane = jnp.where(slab == slabs - 1, ghost_high, from_above.astype(jnp.float32))
        partial = lax.dot_general(
            current, down_factor, (((0,), (0,)), ((), ())), preferred_element_type=jnp.float32
        )
        first, second, base = reduce_scatter_rows(
            partial, lambda: transport(params, current, lower_plane, upper_plane)
        )
        coeffs = all_gather_rows(first.astype(jnp.bfloat16), second.astype(jnp.bfloat16))
        current = collide(up_factor, coeffs, base)
    return current.reshape(local_vel, depth, width_x, width_y)


def solution(mesh):
    return jax.shard_map(
        body,
        mesh=mesh,
        in_specs=(P("vel", "space", None, None), P("vel", None), P("vel", None), P("vel"), P()),
        out_specs=P("vel", "space", None, None),
        check_vma=False,
    )
```

```python
import functools

import jax
import jax.numpy as jnp
from jax import lax
from jax.experimental import pallas as pl
from jax.experimental.pallas import tpu as pltpu
from jax.sharding import PartitionSpec as P


NV = 16
STEPS = 2


speed_range = 8.0
time_ratio = 0.08
wall_heat = 3.0


def components(vel_ids):
    spacing = speed_range / NV
    midpoint = (NV - 1) / 2.0
    along_z = ((vel_ids // (NV * NV)).astype(jnp.float32) - midpoint) * spacing
    along_x = ((vel_ids // NV % NV).astype(jnp.float32) - midpoint) * spacing
    along_y = ((vel_ids % NV).astype(jnp.float32) - midpoint) * spacing
    return (along_z, along_x, along_y)


def wall_ghost(outflux, kind_face, maxwell, energy, norm):
    sigma = outflux / norm
    heating = jnp.where(kind_face == 1, wall_heat, 0.0)
    opened = jnp.where(kind_face == 2, 0.0, 1.0)
    return (
        maxwell[:, None]
        * (sigma[None] + heating[None] * energy[:, None])
        * opened[None]
    )


def transport_kernel(par_ref, cur_ref, lo_ref, hi_ref, out_ref, work_ref, *, depth, plane, width):
    work_ref[:, 0:plane] = lo_ref[...]
    work_ref[:, (depth + 1) * plane:(depth + 2) * plane] = hi_ref[...]
    work_ref[:, plane:(depth + 1) * plane] = cur_ref[...].astype(jnp.float32)
    rows = plane // width

    def one_plane(z, carry):
        base = pl.multiple_of((z + 1) * plane, plane)
        for x in range(rows):
            at = base + x * width
            xm = base + ((x - 1) % rows) * width
            xp = base + ((x + 1) % rows) * width
            c = work_ref[:, pl.ds(at, width)]
            lo = work_ref[:, pl.ds(at - plane, width)]
            hi = work_ref[:, pl.ds(at + plane, width)]
            left = work_ref[:, pl.ds(xm, width)]
            right = work_ref[:, pl.ds(xp, width)]
            down_y = pltpu.roll(c, 1, 1)
            up_y = pltpu.roll(c, width - 1, 1)
            total = (
                par_ref[0] * c
                + par_ref[1] * lo
                + par_ref[2] * hi
                + par_ref[3] * left
                + par_ref[4] * right
                + par_ref[5] * down_y
                + par_ref[6] * up_y
            )
            out_ref[:, pl.ds(pl.multiple_of(z * plane + x * width, width), width)] = total
        return carry

    lax.fori_loop(0, depth, one_plane, 0)


def collide_kernel(up_ref, coef_a_ref, coef_b_ref, base_ref, out_ref, *, depth, plane):
    up = up_ref[...]
    half = depth // 2

    def planes(coef_ref, first):
        def one_plane(z, carry):
            at = pl.multiple_of(z * plane, plane)
            out_at = pl.multiple_of((z + first) * plane, plane)
            gained = lax.dot_general(
                up, coef_ref[pl.ds(at, plane), :], (((1,), (1,)), ((), ())),
                preferred_element_type=jnp.float32,
            )
            out_ref[:, pl.ds(out_at, plane)] = (
                base_ref[:, pl.ds(out_at, plane)] + time_ratio * gained
            ).astype(out_ref.dtype)
            return carry

        lax.fori_loop(0, coef_ref.shape[0] // plane, one_plane, 0)

    planes(coef_a_ref, 0)
    planes(coef_b_ref, half)


def vel_sum(value):
    count = lax.axis_size("vel")
    hop = 1
    while hop < count:
        value = value + lax.ppermute(value, "vel", [(i, i ^ hop) for i in range(count)])
        hop *= 2
    return value


def halves(value, bit):
    pair = value.reshape((2, value.shape[0] // 2) + value.shape[1:])
    return lax.dynamic_index_in_dim(pair, bit, 0, False), lax.dynamic_index_in_dim(pair, 1 - bit, 0, False)


def joined(mine, theirs, bit):
    return jnp.where(bit == 0, jnp.concatenate([mine, theirs]), jnp.concatenate([theirs, mine]))


def swap(value, hop):
    count = lax.axis_size("vel")
    return lax.ppermute(value, "vel", [(i, i ^ hop) for i in range(count)])


def vel_orders():
    count = lax.axis_size("vel")
    levels = count.bit_length() - 1
    return [1 << b for b in range(1, levels)], [1 << b for b in range(levels - 1, 0, -1)]


def reduce_scatter_rows(value):
    me = lax.axis_index("vel")
    keep, give = halves(value, me % 2)
    value = keep + swap(give, 1)
    first, second = halves(value, 0)
    order_a, order_b = vel_orders()
    for hop_a, hop_b in zip(order_a, order_b):
        keep_a, give_a = halves(first, (me // hop_a) % 2)
        keep_b, give_b = halves(second, (me // hop_b) % 2)
        first = keep_a + swap(give_a, hop_a)
        second = keep_b + swap(give_b, hop_b)
    return first, second


def all_gather_rows(first, second):
    me = lax.axis_index("vel")
    order_a, order_b = vel_orders()
    for hop_a, hop_b in zip(order_a[::-1], order_b[::-1]):
        first = joined(first, swap(first, hop_a), (me // hop_a) % 2)
        second = joined(second, swap(second, hop_b), (me // hop_b) % 2)
    value = jnp.concatenate([first, second])
    return joined(value, swap(value, 1), me % 2)


def body(distribution, up_factor, down_factor, decay, wall_kind):
    local_vel, depth, width_x, width_y = distribution.shape
    plane = width_x * width_y
    cells = depth * plane
    rank = up_factor.shape[1]
    vel_ids = lax.axis_index("vel") * local_vel + jnp.arange(local_vel, dtype=jnp.int32)
    along_z, along_x, along_y = components(vel_ids)
    speed_sq = along_z * along_z + along_x * along_x + along_y * along_y
    maxwell = jnp.exp(-0.5 * speed_sq)
    energy = 0.5 * speed_sq - 1.5
    all_ids = jnp.arange(NV**3, dtype=jnp.int32)
    full_z, full_x, full_y = components(all_ids)
    norm = jnp.sum(
        jnp.maximum(full_z, 0.0)
        * jnp.exp(-0.5 * (full_z * full_z + full_x * full_x + full_y * full_y))
    )
    slab = lax.axis_index("space")
    slabs = lax.axis_size("space")
    dt = time_ratio
    per_vel = jnp.stack(
        [
            1.0 - dt * (jnp.abs(along_z) + jnp.abs(along_x) + jnp.abs(along_y)) - dt * decay,
            dt * jnp.maximum(along_z, 0.0),
            -dt * jnp.minimum(along_z, 0.0),
            dt * jnp.maximum(along_x, 0.0),
            -dt * jnp.minimum(along_x, 0.0),
            dt * jnp.maximum(along_y, 0.0),
            -dt * jnp.minimum(along_y, 0.0),
        ]
    )
    params = jnp.broadcast_to(per_vel[:, :, None], (7, local_vel, width_y))
    wl = jnp.maximum(-along_z, 0.0)
    wh = jnp.maximum(along_z, 0.0)
    count = slabs
    forward = [(i, i + 1) for i in range(count - 1)]
    backward = [(i + 1, i) for i in range(count - 1)]

    vb = 128
    split = (depth // 2) * plane
    transport = pl.pallas_call(
        functools.partial(transport_kernel, depth=depth, plane=plane, width=width_y),
        grid=(local_vel // vb,),
        in_specs=[
            pl.BlockSpec((7, vb, width_y), lambda i: (0, i, 0)),
            pl.BlockSpec((vb, cells), lambda i: (i, 0)),
            pl.BlockSpec((vb, plane), lambda i: (i, 0)),
            pl.BlockSpec((vb, plane), lambda i: (i, 0)),
        ],
        out_specs=pl.BlockSpec((vb, cells), lambda i: (i, 0)),
        out_shape=jax.ShapeDtypeStruct((local_vel, cells), jnp.float32),
        scratch_shapes=[pltpu.VMEM((vb, cells + 2 * plane), jnp.float32)],
        compiler_params=pltpu.CompilerParams(vmem_limit_bytes=48 * 1024 * 1024),
    )
    collide = pl.pallas_call(
        functools.partial(collide_kernel, depth=depth, plane=plane),
        grid=(local_vel // vb,),
        in_specs=[
            pl.BlockSpec((vb, rank), lambda i: (i, 0)),
            pl.BlockSpec((split, rank), lambda i: (0, 0)),
            pl.BlockSpec((cells - split, rank), lambda i: (0, 0)),
            pl.BlockSpec((vb, cells), lambda i: (i, 0)),
        ],
        out_specs=pl.BlockSpec((vb, cells), lambda i: (i, 0)),
        out_shape=jax.ShapeDtypeStruct((local_vel, cells), jnp.bfloat16),
        compiler_params=pltpu.CompilerParams(vmem_limit_bytes=48 * 1024 * 1024),
    )

    current = distribution.reshape(local_vel, cells)
    for step in range(STEPS):
        low_face = current[:, :plane]
        high_face = current[:, cells - plane:]
        out_low = jnp.sum(wl[:, None] * low_face.astype(jnp.float32), axis=0)
        out_high = jnp.sum(wh[:, None] * high_face.astype(jnp.float32), axis=0)
        outflux = vel_sum(jnp.stack([out_low, out_high]))
        ghost_low = wall_ghost(outflux[0], wall_kind[0].reshape(plane), maxwell, energy, norm)
        ghost_high = wall_ghost(outflux[1], wall_kind[1].reshape(plane), maxwell, energy, norm)
        from_below = lax.ppermute(high_face, "space", forward)
        from_above = lax.ppermute(low_face, "space", backward)
        lower_plane = jnp.where(slab == 0, ghost_low, from_below.astype(jnp.float32))
        upper_plane = jnp.where(slab == slabs - 1, ghost_high, from_above.astype(jnp.float32))
        partial = lax.dot_general(
            current, down_factor, (((0,), (0,)), ((), ())), preferred_element_type=jnp.float32
        )
        offloaded = lax.psum_scatter(partial[:split], "vel", scatter_dimension=0, tiled=True)
        first, second = reduce_scatter_rows(partial[split:])
        base = transport(params, current, lower_plane, upper_plane)
        offloaded, first, second, base = lax.optimization_barrier((offloaded, first, second, base))
        coeffs_a = lax.all_gather(offloaded.astype(jnp.bfloat16), "vel", axis=0, tiled=True)
        coeffs_b = all_gather_rows(first.astype(jnp.bfloat16), second.astype(jnp.bfloat16))
        current = collide(up_factor, coeffs_a, coeffs_b, base)
    return current.reshape(local_vel, depth, width_x, width_y)


def solution(mesh):
    return jax.shard_map(
        body,
        mesh=mesh,
        in_specs=(P("vel", "space", None, None), P("vel", None), P("vel", None), P("vel"), P()),
        out_specs=P("vel", "space", None, None),
        check_vma=False,
    )
```

```python
import functools

import jax
import jax.numpy as jnp
from jax import lax
from jax.experimental import pallas as pl
from jax.experimental.pallas import tpu as pltpu
from jax.sharding import PartitionSpec as P


NV = 16
STEPS = 2


speed_range = 8.0
time_ratio = 0.08
wall_heat = 3.0


def components(vel_ids):
    spacing = speed_range / NV
    midpoint = (NV - 1) / 2.0
    along_z = ((vel_ids // (NV * NV)).astype(jnp.float32) - midpoint) * spacing
    along_x = ((vel_ids // NV % NV).astype(jnp.float32) - midpoint) * spacing
    along_y = ((vel_ids % NV).astype(jnp.float32) - midpoint) * spacing
    return (along_z, along_x, along_y)


def wall_ghost(outflux, kind_face, maxwell, energy, norm):
    sigma = outflux / norm
    heating = jnp.where(kind_face == 1, wall_heat, 0.0)
    opened = jnp.where(kind_face == 2, 0.0, 1.0)
    return (
        maxwell[:, None]
        * (sigma[None] + heating[None] * energy[:, None])
        * opened[None]
    )


def transport_kernel(par_ref, cur_ref, lo_ref, hi_ref, out_ref, work_ref, *, depth, plane, width):
    work_ref[:, 0:plane] = lo_ref[...]
    work_ref[:, (depth + 1) * plane:(depth + 2) * plane] = hi_ref[...]
    work_ref[:, plane:(depth + 1) * plane] = cur_ref[...].astype(jnp.float32)
    rows = plane // width

    def one_plane(z, carry):
        base = pl.multiple_of((z + 1) * plane, plane)
        for x in range(rows):
            at = base + x * width
            xm = base + ((x - 1) % rows) * width
            xp = base + ((x + 1) % rows) * width
            c = work_ref[:, pl.ds(at, width)]
            lo = work_ref[:, pl.ds(at - plane, width)]
            hi = work_ref[:, pl.ds(at + plane, width)]
            left = work_ref[:, pl.ds(xm, width)]
            right = work_ref[:, pl.ds(xp, width)]
            down_y = pltpu.roll(c, 1, 1)
            up_y = pltpu.roll(c, width - 1, 1)
            total = (
                par_ref[0] * c
                + par_ref[1] * lo
                + par_ref[2] * hi
                + par_ref[3] * left
                + par_ref[4] * right
                + par_ref[5] * down_y
                + par_ref[6] * up_y
            )
            out_ref[:, pl.ds(pl.multiple_of(z * plane + x * width, width), width)] = total
        return carry

    lax.fori_loop(0, depth, one_plane, 0)


def collide_kernel(up_ref, coef_ref, base_ref, *rest, plane):
    out_ref = rest[-1]
    up = up_ref[...]

    def one_plane(z, carry):
        at = pl.multiple_of(z * plane, plane)
        gained = lax.dot_general(
            up, coef_ref[pl.ds(at, plane), :], (((1,), (1,)), ((), ())),
            preferred_element_type=jnp.float32,
        )
        out_ref[:, pl.ds(at, plane)] = (base_ref[:, pl.ds(at, plane)] + time_ratio * gained).astype(out_ref.dtype)
        return carry

    lax.fori_loop(0, coef_ref.shape[0] // plane, one_plane, 0)


def vel_sum(value):
    count = lax.axis_size("vel")
    hop = 1
    while hop < count:
        value = value + lax.ppermute(value, "vel", [(i, i ^ hop) for i in range(count)])
        hop *= 2
    return value


def halves(value, bit):
    pair = value.reshape((2, value.shape[0] // 2) + value.shape[1:])
    return lax.dynamic_index_in_dim(pair, bit, 0, False), lax.dynamic_index_in_dim(pair, 1 - bit, 0, False)


def joined(mine, theirs, bit):
    return jnp.where(bit == 0, jnp.concatenate([mine, theirs]), jnp.concatenate([theirs, mine]))


def swap(value, hop):
    count = lax.axis_size("vel")
    return lax.ppermute(value, "vel", [(i, i ^ hop) for i in range(count)])


def vel_orders():
    count = lax.axis_size("vel")
    levels = count.bit_length() - 1
    return [1 << b for b in range(1, levels)], [1 << b for b in range(levels - 1, 0, -1)]


def reduce_scatter_rows(value):
    me = lax.axis_index("vel")
    keep, give = halves(value, me % 2)
    value = keep + swap(give, 1)
    first, second = halves(value, 0)
    order_a, order_b = vel_orders()
    for hop_a, hop_b in zip(order_a, order_b):
        keep_a, give_a = halves(first, (me // hop_a) % 2)
        keep_b, give_b = halves(second, (me // hop_b) % 2)
        first = keep_a + swap(give_a, hop_a)
        second = keep_b + swap(give_b, hop_b)
    return first, second


def all_gather_rows(first, second):
    me = lax.axis_index("vel")
    order_a, order_b = vel_orders()
    for hop_a, hop_b in zip(order_a[::-1], order_b[::-1]):
        first = joined(first, swap(first, hop_a), (me // hop_a) % 2)
        second = joined(second, swap(second, hop_b), (me // hop_b) % 2)
    value = jnp.concatenate([first, second])
    return joined(value, swap(value, 1), me % 2)


def body(distribution, up_factor, down_factor, decay, wall_kind):
    local_vel, depth, width_x, width_y = distribution.shape
    plane = width_x * width_y
    cells = depth * plane
    rank = up_factor.shape[1]
    vel_ids = lax.axis_index("vel") * local_vel + jnp.arange(local_vel, dtype=jnp.int32)
    along_z, along_x, along_y = components(vel_ids)
    speed_sq = along_z * along_z + along_x * along_x + along_y * along_y
    maxwell = jnp.exp(-0.5 * speed_sq)
    energy = 0.5 * speed_sq - 1.5
    all_ids = jnp.arange(NV**3, dtype=jnp.int32)
    full_z, full_x, full_y = components(all_ids)
    norm = jnp.sum(
        jnp.maximum(full_z, 0.0)
        * jnp.exp(-0.5 * (full_z * full_z + full_x * full_x + full_y * full_y))
    )
    slab = lax.axis_index("space")
    slabs = lax.axis_size("space")
    dt = time_ratio
    per_vel = jnp.stack(
        [
            1.0 - dt * (jnp.abs(along_z) + jnp.abs(along_x) + jnp.abs(along_y)) - dt * decay,
            dt * jnp.maximum(along_z, 0.0),
            -dt * jnp.minimum(along_z, 0.0),
            dt * jnp.maximum(along_x, 0.0),
            -dt * jnp.minimum(along_x, 0.0),
            dt * jnp.maximum(along_y, 0.0),
            -dt * jnp.minimum(along_y, 0.0),
        ]
    )
    params = jnp.broadcast_to(per_vel[:, :, None], (7, local_vel, width_y))
    wl = jnp.maximum(-along_z, 0.0)
    wh = jnp.maximum(along_z, 0.0)
    count = slabs
    forward = [(i, i + 1) for i in range(count - 1)]
    backward = [(i + 1, i) for i in range(count - 1)]

    vb = 128
    split = (depth - depth // 3) * plane
    transport = pl.pallas_call(
        functools.partial(transport_kernel, depth=depth, plane=plane, width=width_y),
        grid=(local_vel // vb,),
        in_specs=[
            pl.BlockSpec((7, vb, width_y), lambda i: (0, i, 0)),
            pl.BlockSpec((vb, cells), lambda i: (i, 0)),
            pl.BlockSpec((vb, plane), lambda i: (i, 0)),
            pl.BlockSpec((vb, plane), lambda i: (i, 0)),
        ],
        out_specs=pl.BlockSpec((vb, cells), lambda i: (i, 0)),
        out_shape=jax.ShapeDtypeStruct((local_vel, cells), jnp.float32),
        scratch_shapes=[pltpu.VMEM((vb, cells + 2 * plane), jnp.float32)],
        compiler_params=pltpu.CompilerParams(vmem_limit_bytes=48 * 1024 * 1024),
    )
    tail = cells - split
    collide_head = pl.pallas_call(
        functools.partial(collide_kernel, plane=plane),
        grid=(local_vel // vb,),
        in_specs=[
            pl.BlockSpec((vb, rank), lambda i: (i, 0)),
            pl.BlockSpec((split, rank), lambda i: (0, 0)),
            pl.BlockSpec((vb, split), lambda i: (i, 0)),
        ],
        out_specs=pl.BlockSpec((vb, split), lambda i: (i, 0)),
        out_shape=jax.ShapeDtypeStruct((local_vel, cells), jnp.bfloat16),
        compiler_params=pltpu.CompilerParams(vmem_limit_bytes=48 * 1024 * 1024),
    )
    collide_tail = pl.pallas_call(
        functools.partial(collide_kernel, plane=plane),
        grid=(local_vel // vb,),
        in_specs=[
            pl.BlockSpec((vb, rank), lambda i: (i, 0)),
            pl.BlockSpec((tail, rank), lambda i: (0, 0)),
            pl.BlockSpec((vb, tail), lambda i: (i, split // tail)),
            pl.BlockSpec(memory_space=pl.ANY),
        ],
        out_specs=pl.BlockSpec((vb, tail), lambda i: (i, split // tail)),
        out_shape=jax.ShapeDtypeStruct((local_vel, cells), jnp.bfloat16),
        input_output_aliases={3: 0},
        compiler_params=pltpu.CompilerParams(vmem_limit_bytes=48 * 1024 * 1024),
    )

    current = distribution.reshape(local_vel, cells)
    for step in range(STEPS):
        low_face = current[:, :plane]
        high_face = current[:, cells - plane:]
        out_low = jnp.sum(wl[:, None] * low_face.astype(jnp.float32), axis=0)
        out_high = jnp.sum(wh[:, None] * high_face.astype(jnp.float32), axis=0)
        outflux = vel_sum(jnp.stack([out_low, out_high]))
        ghost_low = wall_ghost(outflux[0], wall_kind[0].reshape(plane), maxwell, energy, norm)
        ghost_high = wall_ghost(outflux[1], wall_kind[1].reshape(plane), maxwell, energy, norm)
        from_below = lax.ppermute(high_face, "space", forward)
        from_above = lax.ppermute(low_face, "space", backward)
        lower_plane = jnp.where(slab == 0, ghost_low, from_below.astype(jnp.float32))
        upper_plane = jnp.where(slab == slabs - 1, ghost_high, from_above.astype(jnp.float32))
        partial = lax.dot_general(
            current, down_factor, (((0,), (0,)), ((), ())), preferred_element_type=jnp.float32
        )
        offloaded = lax.psum_scatter(partial[split:], "vel", scatter_dimension=0, tiled=True)
        first, second = reduce_scatter_rows(partial[:split])
        base = transport(params, current, lower_plane, upper_plane)
        offloaded, first, second, base = lax.optimization_barrier((offloaded, first, second, base))
        coeffs_tail = lax.all_gather(offloaded.astype(jnp.bfloat16), "vel", axis=0, tiled=True)
        coeffs_head = all_gather_rows(first.astype(jnp.bfloat16), second.astype(jnp.bfloat16))
        head = collide_head(up_factor, coeffs_head, base)
        current = collide_tail(up_factor, coeffs_tail, base, head)
    return current.reshape(local_vel, depth, width_x, width_y)


def solution(mesh):
    return jax.shard_map(
        body,
        mesh=mesh,
        in_specs=(P("vel", "space", None, None), P("vel", None), P("vel", None), P("vel"), P()),
        out_specs=P("vel", "space", None, None),
        check_vma=False,
    )
```

```python
import functools

import jax
import jax.numpy as jnp
from jax import lax
from jax.experimental import pallas as pl
from jax.experimental.pallas import tpu as pltpu
from jax.sharding import PartitionSpec as P


NV = 16
STEPS = 2


speed_range = 8.0
time_ratio = 0.08
wall_heat = 3.0


def components(vel_ids):
    spacing = speed_range / NV
    midpoint = (NV - 1) / 2.0
    along_z = ((vel_ids // (NV * NV)).astype(jnp.float32) - midpoint) * spacing
    along_x = ((vel_ids // NV % NV).astype(jnp.float32) - midpoint) * spacing
    along_y = ((vel_ids % NV).astype(jnp.float32) - midpoint) * spacing
    return (along_z, along_x, along_y)


def wall_ghost(outflux, kind_face, maxwell, energy, norm):
    sigma = outflux / norm
    heating = jnp.where(kind_face == 1, wall_heat, 0.0)
    opened = jnp.where(kind_face == 2, 0.0, 1.0)
    return (
        maxwell[:, None]
        * (sigma[None] + heating[None] * energy[:, None])
        * opened[None]
    )


def transport_kernel(par_ref, cur_ref, lo_ref, hi_ref, out_ref, work_ref, *, depth, plane, width):
    work_ref[:, 0:plane] = lo_ref[...]
    work_ref[:, (depth + 1) * plane:(depth + 2) * plane] = hi_ref[...]
    work_ref[:, plane:(depth + 1) * plane] = cur_ref[...].astype(jnp.float32)
    rows = plane // width

    def one_plane(z, carry):
        base = pl.multiple_of((z + 1) * plane, plane)
        for x in range(rows):
            at = base + x * width
            xm = base + ((x - 1) % rows) * width
            xp = base + ((x + 1) % rows) * width
            c = work_ref[:, pl.ds(at, width)]
            lo = work_ref[:, pl.ds(at - plane, width)]
            hi = work_ref[:, pl.ds(at + plane, width)]
            left = work_ref[:, pl.ds(xm, width)]
            right = work_ref[:, pl.ds(xp, width)]
            down_y = pltpu.roll(c, 1, 1)
            up_y = pltpu.roll(c, width - 1, 1)
            total = (
                par_ref[0] * c
                + par_ref[1] * lo
                + par_ref[2] * hi
                + par_ref[3] * left
                + par_ref[4] * right
                + par_ref[5] * down_y
                + par_ref[6] * up_y
            )
            out_ref[:, pl.ds(pl.multiple_of(z * plane + x * width, width), width)] = total
        return carry

    lax.fori_loop(0, depth, one_plane, 0)


def collide_kernel(up_ref, coef_ref, base_ref, out_ref, *, depth, plane):
    up = up_ref[...]

    def one_plane(z, carry):
        at = pl.multiple_of(z * plane, plane)
        gained = jnp.dot(up, coef_ref[:, pl.ds(at, plane)], preferred_element_type=jnp.float32)
        out_ref[:, pl.ds(at, plane)] = (base_ref[:, pl.ds(at, plane)] + time_ratio * gained).astype(out_ref.dtype)
        return carry

    lax.fori_loop(0, depth, one_plane, 0)


def vel_sum(value):
    count = lax.axis_size("vel")
    hop = 1
    while hop < count:
        value = value + lax.ppermute(value, "vel", [(i, i ^ hop) for i in range(count)])
        hop *= 2
    return value


def body(distribution, up_factor, down_factor, decay, wall_kind):
    local_vel, depth, width_x, width_y = distribution.shape
    plane = width_x * width_y
    cells = depth * plane
    rank = up_factor.shape[1]
    vel_ids = lax.axis_index("vel") * local_vel + jnp.arange(local_vel, dtype=jnp.int32)
    along_z, along_x, along_y = components(vel_ids)
    speed_sq = along_z * along_z + along_x * along_x + along_y * along_y
    maxwell = jnp.exp(-0.5 * speed_sq)
    energy = 0.5 * speed_sq - 1.5
    all_ids = jnp.arange(NV**3, dtype=jnp.int32)
    full_z, full_x, full_y = components(all_ids)
    norm = jnp.sum(
        jnp.maximum(full_z, 0.0)
        * jnp.exp(-0.5 * (full_z * full_z + full_x * full_x + full_y * full_y))
    )
    slab = lax.axis_index("space")
    slabs = lax.axis_size("space")
    dt = time_ratio
    per_vel = jnp.stack(
        [
            1.0 - dt * (jnp.abs(along_z) + jnp.abs(along_x) + jnp.abs(along_y)) - dt * decay,
            dt * jnp.maximum(along_z, 0.0),
            -dt * jnp.minimum(along_z, 0.0),
            dt * jnp.maximum(along_x, 0.0),
            -dt * jnp.minimum(along_x, 0.0),
            dt * jnp.maximum(along_y, 0.0),
            -dt * jnp.minimum(along_y, 0.0),
        ]
    )
    params = jnp.broadcast_to(per_vel[:, :, None], (7, local_vel, width_y))
    wl = jnp.maximum(-along_z, 0.0)
    wh = jnp.maximum(along_z, 0.0)
    count = slabs
    forward = [(i, i + 1) for i in range(count - 1)]
    backward = [(i + 1, i) for i in range(count - 1)]

    vb = 128
    transport = pl.pallas_call(
        functools.partial(transport_kernel, depth=depth, plane=plane, width=width_y),
        grid=(local_vel // vb,),
        in_specs=[
            pl.BlockSpec((7, vb, width_y), lambda i: (0, i, 0)),
            pl.BlockSpec((vb, cells), lambda i: (i, 0)),
            pl.BlockSpec((vb, plane), lambda i: (i, 0)),
            pl.BlockSpec((vb, plane), lambda i: (i, 0)),
        ],
        out_specs=pl.BlockSpec((vb, cells), lambda i: (i, 0)),
        out_shape=jax.ShapeDtypeStruct((local_vel, cells), jnp.float32),
        scratch_shapes=[pltpu.VMEM((vb, cells + 2 * plane), jnp.float32)],
        compiler_params=pltpu.CompilerParams(vmem_limit_bytes=48 * 1024 * 1024),
    )
    collide = pl.pallas_call(
        functools.partial(collide_kernel, depth=depth, plane=plane),
        grid=(local_vel // vb,),
        in_specs=[
            pl.BlockSpec((vb, rank), lambda i: (i, 0)),
            pl.BlockSpec((rank, cells), lambda i: (0, 0)),
            pl.BlockSpec((vb, cells), lambda i: (i, 0)),
        ],
        out_specs=pl.BlockSpec((vb, cells), lambda i: (i, 0)),
        out_shape=jax.ShapeDtypeStruct((local_vel, cells), jnp.bfloat16),
        compiler_params=pltpu.CompilerParams(vmem_limit_bytes=48 * 1024 * 1024),
    )

    current = distribution.reshape(local_vel, cells)
    for step in range(STEPS):
        low_face = current[:, :plane]
        high_face = current[:, cells - plane:]
        out_low = jnp.sum(wl[:, None] * low_face.astype(jnp.float32), axis=0)
        out_high = jnp.sum(wh[:, None] * high_face.astype(jnp.float32), axis=0)
        outflux = vel_sum(jnp.stack([out_low, out_high]))
        ghost_low = wall_ghost(outflux[0], wall_kind[0].reshape(plane), maxwell, energy, norm)
        ghost_high = wall_ghost(outflux[1], wall_kind[1].reshape(plane), maxwell, energy, norm)
        from_below = lax.ppermute(high_face, "space", forward)
        from_above = lax.ppermute(low_face, "space", backward)
        lower_plane = jnp.where(slab == 0, ghost_low, from_below.astype(jnp.float32))
        upper_plane = jnp.where(slab == slabs - 1, ghost_high, from_above.astype(jnp.float32))
        partial = lax.dot_general(
            down_factor, current, (((0,), (0,)), ((), ())), preferred_element_type=jnp.float32
        )
        coeffs = lax.psum_scatter(partial, "vel", scatter_dimension=0, tiled=True)
        base = transport(params, current, lower_plane, upper_plane)
        coeffs, base = lax.optimization_barrier((coeffs, base))
        coeffs = lax.all_gather(coeffs.astype(jnp.bfloat16), "vel", axis=0, tiled=True)
        current = collide(up_factor, coeffs, base)
    return current.reshape(local_vel, depth, width_x, width_y)


def solution(mesh):
    return jax.shard_map(
        body,
        mesh=mesh,
        in_specs=(P("vel", "space", None, None), P("vel", None), P("vel", None), P("vel"), P()),
        out_specs=P("vel", "space", None, None),
        check_vma=False,
    )
```

```python
import functools

import jax
import jax.numpy as jnp
from jax import lax
from jax.experimental import pallas as pl
from jax.experimental.pallas import tpu as pltpu
from jax.sharding import PartitionSpec as P


NV = 16
STEPS = 2


speed_range = 8.0
time_ratio = 0.08
wall_heat = 3.0


def components(vel_ids):
    spacing = speed_range / NV
    midpoint = (NV - 1) / 2.0
    along_z = ((vel_ids // (NV * NV)).astype(jnp.float32) - midpoint) * spacing
    along_x = ((vel_ids // NV % NV).astype(jnp.float32) - midpoint) * spacing
    along_y = ((vel_ids % NV).astype(jnp.float32) - midpoint) * spacing
    return (along_z, along_x, along_y)


def wall_ghost(outflux, kind_face, maxwell, energy, norm):
    sigma = outflux / norm
    heating = jnp.where(kind_face == 1, wall_heat, 0.0)
    opened = jnp.where(kind_face == 2, 0.0, 1.0)
    return (
        maxwell[:, None]
        * (sigma[None] + heating[None] * energy[:, None])
        * opened[None]
    )


def transport_kernel(par_ref, cur_ref, lo_ref, hi_ref, out_ref, work_ref, *, depth, plane, width):
    work_ref[:, 0:plane] = lo_ref[...]
    work_ref[:, (depth + 1) * plane:(depth + 2) * plane] = hi_ref[...]
    work_ref[:, plane:(depth + 1) * plane] = cur_ref[...].astype(jnp.float32)
    rows = plane // width

    def one_plane(z, carry):
        base = pl.multiple_of((z + 1) * plane, plane)
        for x in range(rows):
            at = base + x * width
            xm = base + ((x - 1) % rows) * width
            xp = base + ((x + 1) % rows) * width
            c = work_ref[:, pl.ds(at, width)]
            lo = work_ref[:, pl.ds(at - plane, width)]
            hi = work_ref[:, pl.ds(at + plane, width)]
            left = work_ref[:, pl.ds(xm, width)]
            right = work_ref[:, pl.ds(xp, width)]
            down_y = pltpu.roll(c, 1, 1)
            up_y = pltpu.roll(c, width - 1, 1)
            total = (
                par_ref[0] * c
                + par_ref[1] * lo
                + par_ref[2] * hi
                + par_ref[3] * left
                + par_ref[4] * right
                + par_ref[5] * down_y
                + par_ref[6] * up_y
            )
            out_ref[:, pl.ds(pl.multiple_of(z * plane + x * width, width), width)] = total
        return carry

    lax.fori_loop(0, depth, one_plane, 0)


def collide_kernel(up_ref, coef_ref, base_ref, out_ref, *, depth, plane):
    up = up_ref[...]

    def one_plane(z, carry):
        at = pl.multiple_of(z * plane, plane)
        gained = jnp.dot(up, coef_ref[:, pl.ds(at, plane)], preferred_element_type=jnp.float32)
        total = base_ref[:, pl.ds(at, plane)] + time_ratio * gained
        if len(out_ref.shape) == 2:
            out_ref[:, pl.ds(at, plane)] = total.astype(out_ref.dtype)
        else:
            shape = (out_ref.shape[0], out_ref.shape[2], out_ref.shape[3])
            out_ref[:, z] = total.reshape(shape).astype(out_ref.dtype)
        return carry

    lax.fori_loop(0, depth, one_plane, 0)


def vel_sum(value):
    count = lax.axis_size("vel")
    hop = 1
    while hop < count:
        value = value + lax.ppermute(value, "vel", [(i, i ^ hop) for i in range(count)])
        hop *= 2
    return value


def body(distribution, up_factor, down_factor, decay, wall_kind):
    local_vel, depth, width_x, width_y = distribution.shape
    plane = width_x * width_y
    cells = depth * plane
    rank = up_factor.shape[1]
    vel_ids = lax.axis_index("vel") * local_vel + jnp.arange(local_vel, dtype=jnp.int32)
    along_z, along_x, along_y = components(vel_ids)
    speed_sq = along_z * along_z + along_x * along_x + along_y * along_y
    maxwell = jnp.exp(-0.5 * speed_sq)
    energy = 0.5 * speed_sq - 1.5
    all_ids = jnp.arange(NV**3, dtype=jnp.int32)
    full_z, full_x, full_y = components(all_ids)
    norm = jnp.sum(
        jnp.maximum(full_z, 0.0)
        * jnp.exp(-0.5 * (full_z * full_z + full_x * full_x + full_y * full_y))
    )
    slab = lax.axis_index("space")
    slabs = lax.axis_size("space")
    dt = time_ratio
    per_vel = jnp.stack(
        [
            1.0 - dt * (jnp.abs(along_z) + jnp.abs(along_x) + jnp.abs(along_y)) - dt * decay,
            dt * jnp.maximum(along_z, 0.0),
            -dt * jnp.minimum(along_z, 0.0),
            dt * jnp.maximum(along_x, 0.0),
            -dt * jnp.minimum(along_x, 0.0),
            dt * jnp.maximum(along_y, 0.0),
            -dt * jnp.minimum(along_y, 0.0),
        ]
    )
    params = jnp.broadcast_to(per_vel[:, :, None], (7, local_vel, width_y))
    wl = jnp.maximum(-along_z, 0.0)
    wh = jnp.maximum(along_z, 0.0)
    count = slabs
    forward = [(i, i + 1) for i in range(count - 1)]
    backward = [(i + 1, i) for i in range(count - 1)]

    vb = 128
    transport = pl.pallas_call(
        functools.partial(transport_kernel, depth=depth, plane=plane, width=width_y),
        grid=(local_vel // vb,),
        in_specs=[
            pl.BlockSpec((7, vb, width_y), lambda i: (0, i, 0)),
            pl.BlockSpec((vb, cells), lambda i: (i, 0)),
            pl.BlockSpec((vb, plane), lambda i: (i, 0)),
            pl.BlockSpec((vb, plane), lambda i: (i, 0)),
        ],
        out_specs=pl.BlockSpec((vb, cells), lambda i: (i, 0)),
        out_shape=jax.ShapeDtypeStruct((local_vel, cells), jnp.float32),
        scratch_shapes=[pltpu.VMEM((vb, cells + 2 * plane), jnp.float32)],
        compiler_params=pltpu.CompilerParams(vmem_limit_bytes=48 * 1024 * 1024),
    )
    def collide_call(final):
        if final:
            out_spec = pl.BlockSpec((vb, depth, width_x, width_y), lambda i: (i, 0, 0, 0))
            out_shape = jax.ShapeDtypeStruct((local_vel, depth, width_x, width_y), jnp.bfloat16)
        else:
            out_spec = pl.BlockSpec((vb, cells), lambda i: (i, 0))
            out_shape = jax.ShapeDtypeStruct((local_vel, cells), jnp.bfloat16)
        return pl.pallas_call(
            functools.partial(collide_kernel, depth=depth, plane=plane),
            grid=(local_vel // vb,),
            in_specs=[
                pl.BlockSpec((vb, rank), lambda i: (i, 0)),
                pl.BlockSpec((rank, cells), lambda i: (0, 0)),
                pl.BlockSpec((vb, cells), lambda i: (i, 0)),
            ],
            out_specs=out_spec,
            out_shape=out_shape,
            compiler_params=pltpu.CompilerParams(vmem_limit_bytes=48 * 1024 * 1024),
        )

    current = distribution.reshape(local_vel, cells)
    for step in range(STEPS):
        low_face = current[:, :plane]
        high_face = current[:, cells - plane:]
        out_low = jnp.sum(wl[:, None] * low_face.astype(jnp.float32), axis=0)
        out_high = jnp.sum(wh[:, None] * high_face.astype(jnp.float32), axis=0)
        outflux = vel_sum(jnp.stack([out_low, out_high]))
        ghost_low = wall_ghost(outflux[0], wall_kind[0].reshape(plane), maxwell, energy, norm)
        ghost_high = wall_ghost(outflux[1], wall_kind[1].reshape(plane), maxwell, energy, norm)
        from_below = lax.ppermute(high_face, "space", forward)
        from_above = lax.ppermute(low_face, "space", backward)
        lower_plane = jnp.where(slab == 0, ghost_low, from_below.astype(jnp.float32))
        upper_plane = jnp.where(slab == slabs - 1, ghost_high, from_above.astype(jnp.float32))
        partial = lax.dot_general(
            down_factor, current, (((0,), (0,)), ((), ())), preferred_element_type=jnp.float32
        )
        coeffs = lax.psum_scatter(partial, "vel", scatter_dimension=0, tiled=True)
        base = transport(params, current, lower_plane, upper_plane)
        coeffs, base = lax.optimization_barrier((coeffs, base))
        coeffs = lax.all_gather(coeffs.astype(jnp.bfloat16), "vel", axis=0, tiled=True)
        current = collide_call(step == STEPS - 1)(up_factor, coeffs, base)
    return current


def solution(mesh):
    return jax.shard_map(
        body,
        mesh=mesh,
        in_specs=(P("vel", "space", None, None), P("vel", None), P("vel", None), P("vel"), P()),
        out_specs=P("vel", "space", None, None),
        check_vma=False,
    )
```

```python
import functools

import jax
import jax.numpy as jnp
from jax import lax
from jax.experimental import pallas as pl
from jax.experimental.pallas import tpu as pltpu
from jax.sharding import PartitionSpec as P


NV = 16
STEPS = 2


speed_range = 8.0
time_ratio = 0.08
wall_heat = 3.0


def components(vel_ids):
    spacing = speed_range / NV
    midpoint = (NV - 1) / 2.0
    along_z = ((vel_ids // (NV * NV)).astype(jnp.float32) - midpoint) * spacing
    along_x = ((vel_ids // NV % NV).astype(jnp.float32) - midpoint) * spacing
    along_y = ((vel_ids % NV).astype(jnp.float32) - midpoint) * spacing
    return (along_z, along_x, along_y)


def wall_ghost(outflux, kind_face, maxwell, energy, norm):
    sigma = outflux / norm
    heating = jnp.where(kind_face == 1, wall_heat, 0.0)
    opened = jnp.where(kind_face == 2, 0.0, 1.0)
    return (
        maxwell[:, None]
        * (sigma[None] + heating[None] * energy[:, None])
        * opened[None]
    )


def transport_kernel(par_ref, cur_ref, lo_ref, hi_ref, out_ref, work_ref, *, depth, plane, width):
    work_ref[:, 0:plane] = lo_ref[...]
    work_ref[:, (depth + 1) * plane:(depth + 2) * plane] = hi_ref[...]
    work_ref[:, plane:(depth + 1) * plane] = cur_ref[...].astype(jnp.float32)
    rows = plane // width

    def one_plane(z, carry):
        base = pl.multiple_of((z + 1) * plane, plane)
        for x in range(rows):
            at = base + x * width
            xm = base + ((x - 1) % rows) * width
            xp = base + ((x + 1) % rows) * width
            c = work_ref[:, pl.ds(at, width)]
            lo = work_ref[:, pl.ds(at - plane, width)]
            hi = work_ref[:, pl.ds(at + plane, width)]
            left = work_ref[:, pl.ds(xm, width)]
            right = work_ref[:, pl.ds(xp, width)]
            down_y = pltpu.roll(c, 1, 1)
            up_y = pltpu.roll(c, width - 1, 1)
            total = (
                par_ref[0] * c
                + par_ref[1] * lo
                + par_ref[2] * hi
                + par_ref[3] * left
                + par_ref[4] * right
                + par_ref[5] * down_y
                + par_ref[6] * up_y
            )
            out_ref[:, pl.ds(pl.multiple_of(z * plane + x * width, width), width)] = total
        return carry

    lax.fori_loop(0, depth, one_plane, 0)


def collide_kernel(up_ref, coef_ref, base_ref, out_ref):
    gained = jnp.dot(up_ref[...], coef_ref[...], preferred_element_type=jnp.float32)
    total = base_ref[...] + time_ratio * gained
    if len(out_ref.shape) == 2:
        out_ref[...] = total.astype(out_ref.dtype)
    else:
        shape = (out_ref.shape[0], out_ref.shape[2], out_ref.shape[3])
        out_ref[:, 0] = total.reshape(shape).astype(out_ref.dtype)


def vel_sum(value):
    count = lax.axis_size("vel")
    hop = 1
    while hop < count:
        value = value + lax.ppermute(value, "vel", [(i, i ^ hop) for i in range(count)])
        hop *= 2
    return value


def body(distribution, up_factor, down_factor, decay, wall_kind):
    local_vel, depth, width_x, width_y = distribution.shape
    plane = width_x * width_y
    cells = depth * plane
    rank = up_factor.shape[1]
    vel_ids = lax.axis_index("vel") * local_vel + jnp.arange(local_vel, dtype=jnp.int32)
    along_z, along_x, along_y = components(vel_ids)
    speed_sq = along_z * along_z + along_x * along_x + along_y * along_y
    maxwell = jnp.exp(-0.5 * speed_sq)
    energy = 0.5 * speed_sq - 1.5
    all_ids = jnp.arange(NV**3, dtype=jnp.int32)
    full_z, full_x, full_y = components(all_ids)
    norm = jnp.sum(
        jnp.maximum(full_z, 0.0)
        * jnp.exp(-0.5 * (full_z * full_z + full_x * full_x + full_y * full_y))
    )
    slab = lax.axis_index("space")
    slabs = lax.axis_size("space")
    dt = time_ratio
    per_vel = jnp.stack(
        [
            1.0 - dt * (jnp.abs(along_z) + jnp.abs(along_x) + jnp.abs(along_y)) - dt * decay,
            dt * jnp.maximum(along_z, 0.0),
            -dt * jnp.minimum(along_z, 0.0),
            dt * jnp.maximum(along_x, 0.0),
            -dt * jnp.minimum(along_x, 0.0),
            dt * jnp.maximum(along_y, 0.0),
            -dt * jnp.minimum(along_y, 0.0),
        ]
    )
    params = jnp.broadcast_to(per_vel[:, :, None], (7, local_vel, width_y))
    wl = jnp.maximum(-along_z, 0.0)
    wh = jnp.maximum(along_z, 0.0)
    count = slabs
    forward = [(i, i + 1) for i in range(count - 1)]
    backward = [(i + 1, i) for i in range(count - 1)]

    vb = 128
    transport = pl.pallas_call(
        functools.partial(transport_kernel, depth=depth, plane=plane, width=width_y),
        grid=(local_vel // vb,),
        in_specs=[
            pl.BlockSpec((7, vb, width_y), lambda i: (0, i, 0)),
            pl.BlockSpec((vb, cells), lambda i: (i, 0)),
            pl.BlockSpec((vb, plane), lambda i: (i, 0)),
            pl.BlockSpec((vb, plane), lambda i: (i, 0)),
        ],
        out_specs=pl.BlockSpec((vb, cells), lambda i: (i, 0)),
        out_shape=jax.ShapeDtypeStruct((local_vel, cells), jnp.float32),
        scratch_shapes=[pltpu.VMEM((vb, cells + 2 * plane), jnp.float32)],
        compiler_params=pltpu.CompilerParams(vmem_limit_bytes=48 * 1024 * 1024),
    )
    def collide_call(final):
        if final:
            out_spec = pl.BlockSpec((local_vel, 1, width_x, width_y), lambda z: (0, z, 0, 0))
            out_shape = jax.ShapeDtypeStruct((local_vel, depth, width_x, width_y), jnp.bfloat16)
        else:
            out_spec = pl.BlockSpec((local_vel, plane), lambda z: (0, z))
            out_shape = jax.ShapeDtypeStruct((local_vel, cells), jnp.bfloat16)
        return pl.pallas_call(
            collide_kernel,
            grid=(depth,),
            in_specs=[
                pl.BlockSpec((local_vel, rank), lambda z: (0, 0)),
                pl.BlockSpec((rank, plane), lambda z: (0, z)),
                pl.BlockSpec((local_vel, plane), lambda z: (0, z)),
            ],
            out_specs=out_spec,
            out_shape=out_shape,
            compiler_params=pltpu.CompilerParams(vmem_limit_bytes=48 * 1024 * 1024),
        )

    current = distribution.reshape(local_vel, cells)
    for step in range(STEPS):
        low_face = current[:, :plane]
        high_face = current[:, cells - plane:]
        out_low = jnp.sum(wl[:, None] * low_face.astype(jnp.float32), axis=0)
        out_high = jnp.sum(wh[:, None] * high_face.astype(jnp.float32), axis=0)
        outflux = vel_sum(jnp.stack([out_low, out_high]))
        ghost_low = wall_ghost(outflux[0], wall_kind[0].reshape(plane), maxwell, energy, norm)
        ghost_high = wall_ghost(outflux[1], wall_kind[1].reshape(plane), maxwell, energy, norm)
        from_below = lax.ppermute(high_face, "space", forward)
        from_above = lax.ppermute(low_face, "space", backward)
        lower_plane = jnp.where(slab == 0, ghost_low, from_below.astype(jnp.float32))
        upper_plane = jnp.where(slab == slabs - 1, ghost_high, from_above.astype(jnp.float32))
        partial = lax.dot_general(
            down_factor, current, (((0,), (0,)), ((), ())), preferred_element_type=jnp.float32
        )
        coeffs = lax.psum_scatter(partial, "vel", scatter_dimension=0, tiled=True)
        base = transport(params, current, lower_plane, upper_plane)
        coeffs, base = lax.optimization_barrier((coeffs, base))
        coeffs = lax.all_gather(coeffs.astype(jnp.bfloat16), "vel", axis=0, tiled=True)
        current = collide_call(step == STEPS - 1)(up_factor, coeffs, base)
    return current


def solution(mesh):
    return jax.shard_map(
        body,
        mesh=mesh,
        in_specs=(P("vel", "space", None, None), P("vel", None), P("vel", None), P("vel"), P()),
        out_specs=P("vel", "space", None, None),
        check_vma=False,
    )
```

```python
import functools

import jax
import jax.numpy as jnp
from jax import lax
from jax.experimental import pallas as pl
from jax.experimental.pallas import tpu as pltpu
from jax.sharding import PartitionSpec as P


NV = 16
STEPS = 2


speed_range = 8.0
time_ratio = 0.08
wall_heat = 3.0


def components(vel_ids):
    spacing = speed_range / NV
    midpoint = (NV - 1) / 2.0
    along_z = ((vel_ids // (NV * NV)).astype(jnp.float32) - midpoint) * spacing
    along_x = ((vel_ids // NV % NV).astype(jnp.float32) - midpoint) * spacing
    along_y = ((vel_ids % NV).astype(jnp.float32) - midpoint) * spacing
    return (along_z, along_x, along_y)


def wall_ghost(outflux, kind_face, maxwell, energy, norm):
    sigma = outflux / norm
    heating = jnp.where(kind_face == 1, wall_heat, 0.0)
    opened = jnp.where(kind_face == 2, 0.0, 1.0)
    return (
        maxwell[:, None]
        * (sigma[None] + heating[None] * energy[:, None])
        * opened[None]
    )


def transport_kernel(par_ref, cur_ref, lo_ref, hi_ref, out_ref, work_ref, *, depth, plane, width):
    work_ref[:, 0:plane] = lo_ref[...]
    work_ref[:, (depth + 1) * plane:(depth + 2) * plane] = hi_ref[...]
    work_ref[:, plane:(depth + 1) * plane] = cur_ref[...].astype(jnp.float32)
    rows = plane // width

    def one_plane(z, carry):
        base = pl.multiple_of((z + 1) * plane, plane)
        for x in range(rows):
            at = base + x * width
            xm = base + ((x - 1) % rows) * width
            xp = base + ((x + 1) % rows) * width
            c = work_ref[:, pl.ds(at, width)]
            lo = work_ref[:, pl.ds(at - plane, width)]
            hi = work_ref[:, pl.ds(at + plane, width)]
            left = work_ref[:, pl.ds(xm, width)]
            right = work_ref[:, pl.ds(xp, width)]
            down_y = pltpu.roll(c, 1, 1)
            up_y = pltpu.roll(c, width - 1, 1)
            total = (
                par_ref[0] * c
                + par_ref[1] * lo
                + par_ref[2] * hi
                + par_ref[3] * left
                + par_ref[4] * right
                + par_ref[5] * down_y
                + par_ref[6] * up_y
            )
            out_ref[:, pl.ds(pl.multiple_of(z * plane + x * width, width), width)] = total
        return carry

    lax.fori_loop(0, depth, one_plane, 0)


def collide_kernel(up_ref, coef_ref, base_ref, *rest):
    gained = jnp.dot(up_ref[...], coef_ref[...], preferred_element_type=jnp.float32)
    total = base_ref[...] + time_ratio * gained
    if len(rest) == 1:
        out_ref = rest[0]
        shape = (out_ref.shape[0], out_ref.shape[2], out_ref.shape[3])
        out_ref[:, 0] = total.reshape(shape).astype(out_ref.dtype)
    else:
        down_t_ref, out_ref, partial_ref = rest
        stored = total.astype(out_ref.dtype)
        out_ref[...] = stored
        partial_ref[...] = jnp.dot(down_t_ref[...], stored, preferred_element_type=jnp.float32)


def vel_sum(value):
    count = lax.axis_size("vel")
    hop = 1
    while hop < count:
        value = value + lax.ppermute(value, "vel", [(i, i ^ hop) for i in range(count)])
        hop *= 2
    return value


def body(distribution, up_factor, down_factor, decay, wall_kind):
    local_vel, depth, width_x, width_y = distribution.shape
    plane = width_x * width_y
    cells = depth * plane
    rank = up_factor.shape[1]
    vel_ids = lax.axis_index("vel") * local_vel + jnp.arange(local_vel, dtype=jnp.int32)
    along_z, along_x, along_y = components(vel_ids)
    speed_sq = along_z * along_z + along_x * along_x + along_y * along_y
    maxwell = jnp.exp(-0.5 * speed_sq)
    energy = 0.5 * speed_sq - 1.5
    all_ids = jnp.arange(NV**3, dtype=jnp.int32)
    full_z, full_x, full_y = components(all_ids)
    norm = jnp.sum(
        jnp.maximum(full_z, 0.0)
        * jnp.exp(-0.5 * (full_z * full_z + full_x * full_x + full_y * full_y))
    )
    slab = lax.axis_index("space")
    slabs = lax.axis_size("space")
    dt = time_ratio
    per_vel = jnp.stack(
        [
            1.0 - dt * (jnp.abs(along_z) + jnp.abs(along_x) + jnp.abs(along_y)) - dt * decay,
            dt * jnp.maximum(along_z, 0.0),
            -dt * jnp.minimum(along_z, 0.0),
            dt * jnp.maximum(along_x, 0.0),
            -dt * jnp.minimum(along_x, 0.0),
            dt * jnp.maximum(along_y, 0.0),
            -dt * jnp.minimum(along_y, 0.0),
        ]
    )
    params = jnp.broadcast_to(per_vel[:, :, None], (7, local_vel, width_y))
    wl = jnp.maximum(-along_z, 0.0)
    wh = jnp.maximum(along_z, 0.0)
    count = slabs
    forward = [(i, i + 1) for i in range(count - 1)]
    backward = [(i + 1, i) for i in range(count - 1)]

    vb = 128
    transport = pl.pallas_call(
        functools.partial(transport_kernel, depth=depth, plane=plane, width=width_y),
        grid=(local_vel // vb,),
        in_specs=[
            pl.BlockSpec((7, vb, width_y), lambda i: (0, i, 0)),
            pl.BlockSpec((vb, cells), lambda i: (i, 0)),
            pl.BlockSpec((vb, plane), lambda i: (i, 0)),
            pl.BlockSpec((vb, plane), lambda i: (i, 0)),
        ],
        out_specs=pl.BlockSpec((vb, cells), lambda i: (i, 0)),
        out_shape=jax.ShapeDtypeStruct((local_vel, cells), jnp.float32),
        scratch_shapes=[pltpu.VMEM((vb, cells + 2 * plane), jnp.float32)],
        compiler_params=pltpu.CompilerParams(vmem_limit_bytes=48 * 1024 * 1024),
    )
    def collide_call(final):
        in_specs = [
            pl.BlockSpec((local_vel, rank), lambda z: (0, 0)),
            pl.BlockSpec((rank, plane), lambda z: (0, z)),
            pl.BlockSpec((local_vel, plane), lambda z: (0, z)),
        ]
        if final:
            out_specs = pl.BlockSpec((local_vel, 1, width_x, width_y), lambda z: (0, z, 0, 0))
            out_shape = jax.ShapeDtypeStruct((local_vel, depth, width_x, width_y), jnp.bfloat16)
        else:
            in_specs.append(pl.BlockSpec((rank, local_vel), lambda z: (0, 0)))
            out_specs = [
                pl.BlockSpec((local_vel, plane), lambda z: (0, z)),
                pl.BlockSpec((rank, plane), lambda z: (0, z)),
            ]
            out_shape = [
                jax.ShapeDtypeStruct((local_vel, cells), jnp.bfloat16),
                jax.ShapeDtypeStruct((rank, cells), jnp.float32),
            ]
        return pl.pallas_call(
            collide_kernel,
            grid=(depth,),
            in_specs=in_specs,
            out_specs=out_specs,
            out_shape=out_shape,
            compiler_params=pltpu.CompilerParams(vmem_limit_bytes=48 * 1024 * 1024),
        )

    current = distribution.reshape(local_vel, cells)
    down_t = down_factor.T
    partial = lax.dot_general(
        down_factor, current, (((0,), (0,)), ((), ())), preferred_element_type=jnp.float32
    )
    for step in range(STEPS):
        low_face = current[:, :plane]
        high_face = current[:, cells - plane:]
        out_low = jnp.sum(wl[:, None] * low_face.astype(jnp.float32), axis=0)
        out_high = jnp.sum(wh[:, None] * high_face.astype(jnp.float32), axis=0)
        outflux = vel_sum(jnp.stack([out_low, out_high]))
        ghost_low = wall_ghost(outflux[0], wall_kind[0].reshape(plane), maxwell, energy, norm)
        ghost_high = wall_ghost(outflux[1], wall_kind[1].reshape(plane), maxwell, energy, norm)
        from_below = lax.ppermute(high_face, "space", forward)
        from_above = lax.ppermute(low_face, "space", backward)
        lower_plane = jnp.where(slab == 0, ghost_low, from_below.astype(jnp.float32))
        upper_plane = jnp.where(slab == slabs - 1, ghost_high, from_above.astype(jnp.float32))
        coeffs = lax.psum_scatter(partial, "vel", scatter_dimension=0, tiled=True)
        base = transport(params, current, lower_plane, upper_plane)
        coeffs, base = lax.optimization_barrier((coeffs, base))
        coeffs = lax.all_gather(coeffs.astype(jnp.bfloat16), "vel", axis=0, tiled=True)
        if step == STEPS - 1:
            current = collide_call(True)(up_factor, coeffs, base)
        else:
            current, partial = collide_call(False)(up_factor, coeffs, base, down_t)
    return current


def solution(mesh):
    return jax.shard_map(
        body,
        mesh=mesh,
        in_specs=(P("vel", "space", None, None), P("vel", None), P("vel", None), P("vel"), P()),
        out_specs=P("vel", "space", None, None),
        check_vma=False,
    )
```

```python
import functools

import jax
import jax.numpy as jnp
from jax import lax
from jax.experimental import pallas as pl
from jax.experimental.pallas import tpu as pltpu
from jax.sharding import PartitionSpec as P


NV = 16
STEPS = 2


speed_range = 8.0
time_ratio = 0.08
wall_heat = 3.0


def components(vel_ids):
    spacing = speed_range / NV
    midpoint = (NV - 1) / 2.0
    along_z = ((vel_ids // (NV * NV)).astype(jnp.float32) - midpoint) * spacing
    along_x = ((vel_ids // NV % NV).astype(jnp.float32) - midpoint) * spacing
    along_y = ((vel_ids % NV).astype(jnp.float32) - midpoint) * spacing
    return (along_z, along_x, along_y)


def wall_ghost(outflux, kind_face, maxwell, energy, norm):
    sigma = outflux / norm
    heating = jnp.where(kind_face == 1, wall_heat, 0.0)
    opened = jnp.where(kind_face == 2, 0.0, 1.0)
    return (
        maxwell[:, None]
        * (sigma[None] + heating[None] * energy[:, None])
        * opened[None]
    )


def transport_kernel(par_ref, cur_ref, lo_ref, hi_ref, out_ref, work_ref, *, depth, plane, width):
    work_ref[:, 0:plane] = lo_ref[...]
    work_ref[:, (depth + 1) * plane:(depth + 2) * plane] = hi_ref[...]
    work_ref[:, plane:(depth + 1) * plane] = cur_ref[...].astype(jnp.float32)
    rows = plane // width

    def one_plane(z, carry):
        base = pl.multiple_of((z + 1) * plane, plane)
        for x in range(rows):
            at = base + x * width
            xm = base + ((x - 1) % rows) * width
            xp = base + ((x + 1) % rows) * width
            c = work_ref[:, pl.ds(at, width)]
            lo = work_ref[:, pl.ds(at - plane, width)]
            hi = work_ref[:, pl.ds(at + plane, width)]
            left = work_ref[:, pl.ds(xm, width)]
            right = work_ref[:, pl.ds(xp, width)]
            down_y = pltpu.roll(c, 1, 1)
            up_y = pltpu.roll(c, width - 1, 1)
            total = (
                par_ref[0] * c
                + par_ref[1] * lo
                + par_ref[2] * hi
                + par_ref[3] * left
                + par_ref[4] * right
                + par_ref[5] * down_y
                + par_ref[6] * up_y
            )
            out_ref[:, pl.ds(pl.multiple_of(z * plane + x * width, width), width)] = total
        return carry

    lax.fori_loop(0, depth, one_plane, 0)


def collide_kernel(up_ref, coef_ref, base_ref, *rest):
    gained = jnp.dot(up_ref[...], coef_ref[...], preferred_element_type=jnp.float32)
    total = base_ref[...] + time_ratio * gained
    if len(rest) == 1:
        out_ref = rest[0]
        shape = (out_ref.shape[0], out_ref.shape[2], out_ref.shape[3])
        out_ref[:, 0] = total.reshape(shape).astype(out_ref.dtype)
    else:
        down_t_ref, out_ref, partial_ref = rest
        stored = total.astype(out_ref.dtype)
        out_ref[...] = stored
        partial_ref[...] = jnp.dot(down_t_ref[...], stored, preferred_element_type=jnp.float32)


def entry_kernel(cur_ref, down_t_ref, flat_ref, partial_ref):
    value = cur_ref[:, 0].astype(jnp.float32)
    flat = value.reshape(value.shape[0], value.shape[1] * value.shape[2]).astype(flat_ref.dtype)
    flat_ref[...] = flat
    partial_ref[...] = jnp.dot(down_t_ref[...], flat, preferred_element_type=jnp.float32)


def vel_sum(value):
    count = lax.axis_size("vel")
    hop = 1
    while hop < count:
        value = value + lax.ppermute(value, "vel", [(i, i ^ hop) for i in range(count)])
        hop *= 2
    return value


def body(distribution, up_factor, down_factor, decay, wall_kind):
    local_vel, depth, width_x, width_y = distribution.shape
    plane = width_x * width_y
    cells = depth * plane
    rank = up_factor.shape[1]
    vel_ids = lax.axis_index("vel") * local_vel + jnp.arange(local_vel, dtype=jnp.int32)
    along_z, along_x, along_y = components(vel_ids)
    speed_sq = along_z * along_z + along_x * along_x + along_y * along_y
    maxwell = jnp.exp(-0.5 * speed_sq)
    energy = 0.5 * speed_sq - 1.5
    all_ids = jnp.arange(NV**3, dtype=jnp.int32)
    full_z, full_x, full_y = components(all_ids)
    norm = jnp.sum(
        jnp.maximum(full_z, 0.0)
        * jnp.exp(-0.5 * (full_z * full_z + full_x * full_x + full_y * full_y))
    )
    slab = lax.axis_index("space")
    slabs = lax.axis_size("space")
    dt = time_ratio
    per_vel = jnp.stack(
        [
            1.0 - dt * (jnp.abs(along_z) + jnp.abs(along_x) + jnp.abs(along_y)) - dt * decay,
            dt * jnp.maximum(along_z, 0.0),
            -dt * jnp.minimum(along_z, 0.0),
            dt * jnp.maximum(along_x, 0.0),
            -dt * jnp.minimum(along_x, 0.0),
            dt * jnp.maximum(along_y, 0.0),
            -dt * jnp.minimum(along_y, 0.0),
        ]
    )
    params = jnp.broadcast_to(per_vel[:, :, None], (7, local_vel, width_y))
    wl = jnp.maximum(-along_z, 0.0)
    wh = jnp.maximum(along_z, 0.0)
    count = slabs
    forward = [(i, i + 1) for i in range(count - 1)]
    backward = [(i + 1, i) for i in range(count - 1)]

    vb = 128
    transport = pl.pallas_call(
        functools.partial(transport_kernel, depth=depth, plane=plane, width=width_y),
        grid=(local_vel // vb,),
        in_specs=[
            pl.BlockSpec((7, vb, width_y), lambda i: (0, i, 0)),
            pl.BlockSpec((vb, cells), lambda i: (i, 0)),
            pl.BlockSpec((vb, plane), lambda i: (i, 0)),
            pl.BlockSpec((vb, plane), lambda i: (i, 0)),
        ],
        out_specs=pl.BlockSpec((vb, cells), lambda i: (i, 0)),
        out_shape=jax.ShapeDtypeStruct((local_vel, cells), jnp.float32),
        scratch_shapes=[pltpu.VMEM((vb, cells + 2 * plane), jnp.float32)],
        compiler_params=pltpu.CompilerParams(vmem_limit_bytes=48 * 1024 * 1024),
    )
    def collide_call(final):
        in_specs = [
            pl.BlockSpec((local_vel, rank), lambda z: (0, 0)),
            pl.BlockSpec((rank, plane), lambda z: (0, z)),
            pl.BlockSpec((local_vel, plane), lambda z: (0, z)),
        ]
        if final:
            out_specs = pl.BlockSpec((local_vel, 1, width_x, width_y), lambda z: (0, z, 0, 0))
            out_shape = jax.ShapeDtypeStruct((local_vel, depth, width_x, width_y), jnp.bfloat16)
        else:
            in_specs.append(pl.BlockSpec((rank, local_vel), lambda z: (0, 0)))
            out_specs = [
                pl.BlockSpec((local_vel, plane), lambda z: (0, z)),
                pl.BlockSpec((rank, plane), lambda z: (0, z)),
            ]
            out_shape = [
                jax.ShapeDtypeStruct((local_vel, cells), jnp.bfloat16),
                jax.ShapeDtypeStruct((rank, cells), jnp.float32),
            ]
        return pl.pallas_call(
            collide_kernel,
            grid=(depth,),
            in_specs=in_specs,
            out_specs=out_specs,
            out_shape=out_shape,
            compiler_params=pltpu.CompilerParams(vmem_limit_bytes=48 * 1024 * 1024),
        )

    down_t = down_factor.T
    current, partial = pl.pallas_call(
        entry_kernel,
        grid=(depth,),
        in_specs=[
            pl.BlockSpec((local_vel, 1, width_x, width_y), lambda z: (0, z, 0, 0)),
            pl.BlockSpec((rank, local_vel), lambda z: (0, 0)),
        ],
        out_specs=[
            pl.BlockSpec((local_vel, plane), lambda z: (0, z)),
            pl.BlockSpec((rank, plane), lambda z: (0, z)),
        ],
        out_shape=[
            jax.ShapeDtypeStruct((local_vel, cells), jnp.bfloat16),
            jax.ShapeDtypeStruct((rank, cells), jnp.float32),
        ],
        compiler_params=pltpu.CompilerParams(vmem_limit_bytes=48 * 1024 * 1024),
    )(distribution, down_t)
    for step in range(STEPS):
        low_face = current[:, :plane]
        high_face = current[:, cells - plane:]
        out_low = jnp.sum(wl[:, None] * low_face.astype(jnp.float32), axis=0)
        out_high = jnp.sum(wh[:, None] * high_face.astype(jnp.float32), axis=0)
        outflux = vel_sum(jnp.stack([out_low, out_high]))
        ghost_low = wall_ghost(outflux[0], wall_kind[0].reshape(plane), maxwell, energy, norm)
        ghost_high = wall_ghost(outflux[1], wall_kind[1].reshape(plane), maxwell, energy, norm)
        from_below = lax.ppermute(high_face, "space", forward)
        from_above = lax.ppermute(low_face, "space", backward)
        lower_plane = jnp.where(slab == 0, ghost_low, from_below.astype(jnp.float32))
        upper_plane = jnp.where(slab == slabs - 1, ghost_high, from_above.astype(jnp.float32))
        coeffs = lax.psum_scatter(partial, "vel", scatter_dimension=0, tiled=True)
        base = transport(params, current, lower_plane, upper_plane)
        coeffs, base = lax.optimization_barrier((coeffs, base))
        coeffs = lax.all_gather(coeffs.astype(jnp.bfloat16), "vel", axis=0, tiled=True)
        if step == STEPS - 1:
            current = collide_call(True)(up_factor, coeffs, base)
        else:
            current, partial = collide_call(False)(up_factor, coeffs, base, down_t)
    return current


def solution(mesh):
    return jax.shard_map(
        body,
        mesh=mesh,
        in_specs=(P("vel", "space", None, None), P("vel", None), P("vel", None), P("vel"), P()),
        out_specs=P("vel", "space", None, None),
        check_vma=False,
    )
```

```python
import functools

import jax
import jax.numpy as jnp
from jax import lax
from jax.experimental import pallas as pl
from jax.experimental.pallas import tpu as pltpu
from jax.sharding import PartitionSpec as P


NV = 16
STEPS = 2


speed_range = 8.0
time_ratio = 0.08
wall_heat = 3.0


def components(vel_ids):
    spacing = speed_range / NV
    midpoint = (NV - 1) / 2.0
    along_z = ((vel_ids // (NV * NV)).astype(jnp.float32) - midpoint) * spacing
    along_x = ((vel_ids // NV % NV).astype(jnp.float32) - midpoint) * spacing
    along_y = ((vel_ids % NV).astype(jnp.float32) - midpoint) * spacing
    return (along_z, along_x, along_y)


def wall_ghost(outflux, kind_face, maxwell, energy, norm):
    sigma = outflux / norm
    heating = jnp.where(kind_face == 1, wall_heat, 0.0)
    opened = jnp.where(kind_face == 2, 0.0, 1.0)
    return (
        maxwell[:, None]
        * (sigma[None] + heating[None] * energy[:, None])
        * opened[None]
    )


def transport_kernel(par_ref, cur_ref, lo_ref, hi_ref, out_ref, work_ref, *, depth, plane, width):
    work_ref[:, 0:plane] = lo_ref[...]
    work_ref[:, (depth + 1) * plane:(depth + 2) * plane] = hi_ref[...]
    work_ref[:, plane:(depth + 1) * plane] = cur_ref[...].astype(jnp.float32)
    rows = plane // width

    def one_plane(z, carry):
        base = pl.multiple_of((z + 1) * plane, plane)
        for x in range(rows):
            at = base + x * width
            xm = base + ((x - 1) % rows) * width
            xp = base + ((x + 1) % rows) * width
            c = work_ref[:, pl.ds(at, width)]
            lo = work_ref[:, pl.ds(at - plane, width)]
            hi = work_ref[:, pl.ds(at + plane, width)]
            left = work_ref[:, pl.ds(xm, width)]
            right = work_ref[:, pl.ds(xp, width)]
            down_y = pltpu.roll(c, 1, 1)
            up_y = pltpu.roll(c, width - 1, 1)
            total = (
                par_ref[0] * c
                + par_ref[1] * lo
                + par_ref[2] * hi
                + par_ref[3] * left
                + par_ref[4] * right
                + par_ref[5] * down_y
                + par_ref[6] * up_y
            )
            out_ref[:, pl.ds(pl.multiple_of(z * plane + x * width, width), width)] = total
        return carry

    lax.fori_loop(0, depth, one_plane, 0)


def collide_kernel(up_ref, coef_ref, coef_far_ref, base_ref, *rest):
    split = coef_ref.shape[0]
    gained = jnp.dot(up_ref[:, :split], coef_ref[...], preferred_element_type=jnp.float32)
    gained = gained + jnp.dot(up_ref[:, split:], coef_far_ref[...], preferred_element_type=jnp.float32)
    total = base_ref[...] + time_ratio * gained
    if len(rest) == 1:
        out_ref = rest[0]
        shape = (out_ref.shape[0], out_ref.shape[2], out_ref.shape[3])
        out_ref[:, 0] = total.reshape(shape).astype(out_ref.dtype)
    else:
        down_t_ref, out_ref, partial_ref = rest
        stored = total.astype(out_ref.dtype)
        out_ref[...] = stored
        partial_ref[...] = jnp.dot(down_t_ref[...], stored, preferred_element_type=jnp.float32)


def swap(value, hop):
    count = lax.axis_size("vel")
    return lax.ppermute(value, "vel", [(i, i ^ hop) for i in range(count)])


def gather_hops():
    count = lax.axis_size("vel")
    levels = count.bit_length() - 1
    return [1 << b for b in range(levels - 1, 0, -1)], [1 << b for b in range(1, levels)]


def gather_rows(shard):
    half = shard.shape[0] // 2
    first, second = shard[:half], shard[half:]
    for hop_a, hop_b in zip(*gather_hops()):
        first = jnp.concatenate([first, swap(first, hop_a)])
        second = jnp.concatenate([second, swap(second, hop_b)])
    value = jnp.concatenate([first, second])
    return value, swap(value, 1)


def gather_order(rank):
    me = lax.axis_index("vel")
    count = lax.axis_size("vel")
    hops_a, hops_b = gather_hops()
    shard = rank // count
    half = shard // 2
    span = len(hops_a)
    place = jnp.arange(rank, dtype=jnp.int32)
    row = place % half
    pos = (place // half) % (1 << span)
    part = (place // (half << span)) % 2
    source = (place // (half << (span + 1))) ^ (me % 2)
    for k in range(span):
        hop = jnp.where(part == 0, hops_a[k], hops_b[k])
        source = source + (((pos >> k) & 1) ^ ((me // hop) % 2)) * hop
    return source * shard + part * half + row


def vel_sum(value):
    count = lax.axis_size("vel")
    hop = 1
    while hop < count:
        value = value + lax.ppermute(value, "vel", [(i, i ^ hop) for i in range(count)])
        hop *= 2
    return value


def body(distribution, up_factor, down_factor, decay, wall_kind):
    local_vel, depth, width_x, width_y = distribution.shape
    plane = width_x * width_y
    cells = depth * plane
    rank = up_factor.shape[1]
    vel_ids = lax.axis_index("vel") * local_vel + jnp.arange(local_vel, dtype=jnp.int32)
    along_z, along_x, along_y = components(vel_ids)
    speed_sq = along_z * along_z + along_x * along_x + along_y * along_y
    maxwell = jnp.exp(-0.5 * speed_sq)
    energy = 0.5 * speed_sq - 1.5
    all_ids = jnp.arange(NV**3, dtype=jnp.int32)
    full_z, full_x, full_y = components(all_ids)
    norm = jnp.sum(
        jnp.maximum(full_z, 0.0)
        * jnp.exp(-0.5 * (full_z * full_z + full_x * full_x + full_y * full_y))
    )
    slab = lax.axis_index("space")
    slabs = lax.axis_size("space")
    dt = time_ratio
    per_vel = jnp.stack(
        [
            1.0 - dt * (jnp.abs(along_z) + jnp.abs(along_x) + jnp.abs(along_y)) - dt * decay,
            dt * jnp.maximum(along_z, 0.0),
            -dt * jnp.minimum(along_z, 0.0),
            dt * jnp.maximum(along_x, 0.0),
            -dt * jnp.minimum(along_x, 0.0),
            dt * jnp.maximum(along_y, 0.0),
            -dt * jnp.minimum(along_y, 0.0),
        ]
    )
    params = jnp.broadcast_to(per_vel[:, :, None], (7, local_vel, width_y))
    wl = jnp.maximum(-along_z, 0.0)
    wh = jnp.maximum(along_z, 0.0)
    count = slabs
    forward = [(i, i + 1) for i in range(count - 1)]
    backward = [(i + 1, i) for i in range(count - 1)]

    vb = 128
    transport = pl.pallas_call(
        functools.partial(transport_kernel, depth=depth, plane=plane, width=width_y),
        grid=(local_vel // vb,),
        in_specs=[
            pl.BlockSpec((7, vb, width_y), lambda i: (0, i, 0)),
            pl.BlockSpec((vb, cells), lambda i: (i, 0)),
            pl.BlockSpec((vb, plane), lambda i: (i, 0)),
            pl.BlockSpec((vb, plane), lambda i: (i, 0)),
        ],
        out_specs=pl.BlockSpec((vb, cells), lambda i: (i, 0)),
        out_shape=jax.ShapeDtypeStruct((local_vel, cells), jnp.float32),
        scratch_shapes=[pltpu.VMEM((vb, cells + 2 * plane), jnp.float32)],
        compiler_params=pltpu.CompilerParams(vmem_limit_bytes=48 * 1024 * 1024),
    )
    def collide_call(final):
        in_specs = [
            pl.BlockSpec((local_vel, rank), lambda z: (0, 0)),
            pl.BlockSpec((rank // 2, plane), lambda z: (0, z)),
            pl.BlockSpec((rank // 2, plane), lambda z: (0, z)),
            pl.BlockSpec((local_vel, plane), lambda z: (0, z)),
        ]
        if final:
            out_specs = pl.BlockSpec((local_vel, 1, width_x, width_y), lambda z: (0, z, 0, 0))
            out_shape = jax.ShapeDtypeStruct((local_vel, depth, width_x, width_y), jnp.bfloat16)
        else:
            in_specs.append(pl.BlockSpec((rank, local_vel), lambda z: (0, 0)))
            out_specs = [
                pl.BlockSpec((local_vel, plane), lambda z: (0, z)),
                pl.BlockSpec((rank, plane), lambda z: (0, z)),
            ]
            out_shape = [
                jax.ShapeDtypeStruct((local_vel, cells), jnp.bfloat16),
                jax.ShapeDtypeStruct((rank, cells), jnp.float32),
            ]
        return pl.pallas_call(
            collide_kernel,
            grid=(depth,),
            in_specs=in_specs,
            out_specs=out_specs,
            out_shape=out_shape,
            compiler_params=pltpu.CompilerParams(vmem_limit_bytes=48 * 1024 * 1024),
        )

    current = distribution.reshape(local_vel, cells)
    down_t = down_factor.T
    up_order = jnp.take(up_factor, gather_order(rank), axis=1)
    partial = lax.dot_general(
        down_factor, current, (((0,), (0,)), ((), ())), preferred_element_type=jnp.float32
    )
    for step in range(STEPS):
        low_face = current[:, :plane]
        high_face = current[:, cells - plane:]
        out_low = jnp.sum(wl[:, None] * low_face.astype(jnp.float32), axis=0)
        out_high = jnp.sum(wh[:, None] * high_face.astype(jnp.float32), axis=0)
        outflux = vel_sum(jnp.stack([out_low, out_high]))
        ghost_low = wall_ghost(outflux[0], wall_kind[0].reshape(plane), maxwell, energy, norm)
        ghost_high = wall_ghost(outflux[1], wall_kind[1].reshape(plane), maxwell, energy, norm)
        from_below = lax.ppermute(high_face, "space", forward)
        from_above = lax.ppermute(low_face, "space", backward)
        lower_plane = jnp.where(slab == 0, ghost_low, from_below.astype(jnp.float32))
        upper_plane = jnp.where(slab == slabs - 1, ghost_high, from_above.astype(jnp.float32))
        coeffs = lax.psum_scatter(partial, "vel", scatter_dimension=0, tiled=True)
        base = transport(params, current, lower_plane, upper_plane)
        coeffs, base = lax.optimization_barrier((coeffs, base))
        near, far = gather_rows(coeffs.astype(jnp.bfloat16))
        if step == STEPS - 1:
            current = collide_call(True)(up_order, near, far, base)
        else:
            current, partial = collide_call(False)(up_order, near, far, base, down_t)
    return current


def solution(mesh):
    return jax.shard_map(
        body,
        mesh=mesh,
        in_specs=(P("vel", "space", None, None), P("vel", None), P("vel", None), P("vel"), P()),
        out_specs=P("vel", "space", None, None),
        check_vma=False,
    )
```

```python
import functools

import jax
import jax.numpy as jnp
from jax import lax
from jax.experimental import pallas as pl
from jax.experimental.pallas import tpu as pltpu
from jax.sharding import PartitionSpec as P


NV = 16
STEPS = 2


speed_range = 8.0
time_ratio = 0.08
wall_heat = 3.0


def components(vel_ids):
    spacing = speed_range / NV
    midpoint = (NV - 1) / 2.0
    along_z = ((vel_ids // (NV * NV)).astype(jnp.float32) - midpoint) * spacing
    along_x = ((vel_ids // NV % NV).astype(jnp.float32) - midpoint) * spacing
    along_y = ((vel_ids % NV).astype(jnp.float32) - midpoint) * spacing
    return (along_z, along_x, along_y)


def wall_ghost(outflux, kind_face, maxwell, energy, norm):
    sigma = outflux / norm
    heating = jnp.where(kind_face == 1, wall_heat, 0.0)
    opened = jnp.where(kind_face == 2, 0.0, 1.0)
    return (
        maxwell[:, None]
        * (sigma[None] + heating[None] * energy[:, None])
        * opened[None]
    )


def transport_kernel(par_ref, cur_ref, lo_ref, hi_ref, out_ref, work_ref, *, depth, plane, width):
    work_ref[:, 0:plane] = lo_ref[...]
    work_ref[:, (depth + 1) * plane:(depth + 2) * plane] = hi_ref[...]
    work_ref[:, plane:(depth + 1) * plane] = cur_ref[...].astype(jnp.float32)
    rows = plane // width

    def one_plane(z, carry):
        base = pl.multiple_of((z + 1) * plane, plane)
        for x in range(rows):
            at = base + x * width
            xm = base + ((x - 1) % rows) * width
            xp = base + ((x + 1) % rows) * width
            c = work_ref[:, pl.ds(at, width)]
            lo = work_ref[:, pl.ds(at - plane, width)]
            hi = work_ref[:, pl.ds(at + plane, width)]
            left = work_ref[:, pl.ds(xm, width)]
            right = work_ref[:, pl.ds(xp, width)]
            down_y = pltpu.roll(c, 1, 1)
            up_y = pltpu.roll(c, width - 1, 1)
            total = (
                par_ref[0] * c
                + par_ref[1] * lo
                + par_ref[2] * hi
                + par_ref[3] * left
                + par_ref[4] * right
                + par_ref[5] * down_y
                + par_ref[6] * up_y
            )
            out_ref[:, pl.ds(pl.multiple_of(z * plane + x * width, width), width)] = total
        return carry

    lax.fori_loop(0, depth, one_plane, 0)


def collide_kernel(up_ref, *rest):
    coef_refs, base_ref, rest = rest[:4], rest[4], rest[5:]
    part = coef_refs[0].shape[0]
    gained = jnp.dot(up_ref[:, :part], coef_refs[0][...], preferred_element_type=jnp.float32)
    for k in range(1, 4):
        gained = gained + jnp.dot(
            up_ref[:, k * part:(k + 1) * part], coef_refs[k][...], preferred_element_type=jnp.float32
        )
    total = base_ref[...] + time_ratio * gained
    if len(rest) == 1:
        out_ref = rest[0]
        shape = (out_ref.shape[0], out_ref.shape[2], out_ref.shape[3])
        out_ref[:, 0] = total.reshape(shape).astype(out_ref.dtype)
    else:
        down_t_ref, out_ref, partial_ref = rest
        stored = total.astype(out_ref.dtype)
        out_ref[...] = stored
        partial_ref[...] = jnp.dot(down_t_ref[...], stored, preferred_element_type=jnp.float32)


def swap(value, hop):
    count = lax.axis_size("vel")
    return lax.ppermute(value, "vel", [(i, i ^ hop) for i in range(count)])


def gather_hops():
    count = lax.axis_size("vel")
    levels = count.bit_length() - 1
    return [1 << b for b in range(levels - 1, 0, -1)], [1 << b for b in range(1, levels)]


def gather_rows(shard):
    half = shard.shape[0] // 2
    first, second = shard[:half], shard[half:]
    for hop_a, hop_b in zip(*gather_hops()):
        first = jnp.concatenate([first, swap(first, hop_a)])
        second = jnp.concatenate([second, swap(second, hop_b)])
    return first, second, swap(first, 1), swap(second, 1)


def gather_order(rank):
    me = lax.axis_index("vel")
    count = lax.axis_size("vel")
    hops_a, hops_b = gather_hops()
    shard = rank // count
    half = shard // 2
    span = len(hops_a)
    place = jnp.arange(rank, dtype=jnp.int32)
    row = place % half
    pos = (place // half) % (1 << span)
    part = (place // (half << span)) % 2
    source = (place // (half << (span + 1))) ^ (me % 2)
    for k in range(span):
        hop = jnp.where(part == 0, hops_a[k], hops_b[k])
        source = source + (((pos >> k) & 1) ^ ((me // hop) % 2)) * hop
    return source * shard + part * half + row


def vel_sum(value):
    count = lax.axis_size("vel")
    hop = 1
    while hop < count:
        value = value + lax.ppermute(value, "vel", [(i, i ^ hop) for i in range(count)])
        hop *= 2
    return value


def body(distribution, up_factor, down_factor, decay, wall_kind):
    local_vel, depth, width_x, width_y = distribution.shape
    plane = width_x * width_y
    cells = depth * plane
    rank = up_factor.shape[1]
    vel_ids = lax.axis_index("vel") * local_vel + jnp.arange(local_vel, dtype=jnp.int32)
    along_z, along_x, along_y = components(vel_ids)
    speed_sq = along_z * along_z + along_x * along_x + along_y * along_y
    maxwell = jnp.exp(-0.5 * speed_sq)
    energy = 0.5 * speed_sq - 1.5
    all_ids = jnp.arange(NV**3, dtype=jnp.int32)
    full_z, full_x, full_y = components(all_ids)
    norm = jnp.sum(
        jnp.maximum(full_z, 0.0)
        * jnp.exp(-0.5 * (full_z * full_z + full_x * full_x + full_y * full_y))
    )
    slab = lax.axis_index("space")
    slabs = lax.axis_size("space")
    dt = time_ratio
    per_vel = jnp.stack(
        [
            1.0 - dt * (jnp.abs(along_z) + jnp.abs(along_x) + jnp.abs(along_y)) - dt * decay,
            dt * jnp.maximum(along_z, 0.0),
            -dt * jnp.minimum(along_z, 0.0),
            dt * jnp.maximum(along_x, 0.0),
            -dt * jnp.minimum(along_x, 0.0),
            dt * jnp.maximum(along_y, 0.0),
            -dt * jnp.minimum(along_y, 0.0),
        ]
    )
    params = jnp.broadcast_to(per_vel[:, :, None], (7, local_vel, width_y))
    wl = jnp.maximum(-along_z, 0.0)
    wh = jnp.maximum(along_z, 0.0)
    count = slabs
    forward = [(i, i + 1) for i in range(count - 1)]
    backward = [(i + 1, i) for i in range(count - 1)]

    vb = 128
    transport = pl.pallas_call(
        functools.partial(transport_kernel, depth=depth, plane=plane, width=width_y),
        grid=(local_vel // vb,),
        in_specs=[
            pl.BlockSpec((7, vb, width_y), lambda i: (0, i, 0)),
            pl.BlockSpec((vb, cells), lambda i: (i, 0)),
            pl.BlockSpec((vb, plane), lambda i: (i, 0)),
            pl.BlockSpec((vb, plane), lambda i: (i, 0)),
        ],
        out_specs=pl.BlockSpec((vb, cells), lambda i: (i, 0)),
        out_shape=jax.ShapeDtypeStruct((local_vel, cells), jnp.float32),
        scratch_shapes=[pltpu.VMEM((vb, cells + 2 * plane), jnp.float32)],
        compiler_params=pltpu.CompilerParams(vmem_limit_bytes=48 * 1024 * 1024),
    )
    def collide_call(final):
        in_specs = [
            pl.BlockSpec((local_vel, rank), lambda z: (0, 0)),
            pl.BlockSpec((rank // 4, plane), lambda z: (0, z)),
            pl.BlockSpec((rank // 4, plane), lambda z: (0, z)),
            pl.BlockSpec((rank // 4, plane), lambda z: (0, z)),
            pl.BlockSpec((rank // 4, plane), lambda z: (0, z)),
            pl.BlockSpec((local_vel, plane), lambda z: (0, z)),
        ]
        if final:
            out_specs = pl.BlockSpec((local_vel, 1, width_x, width_y), lambda z: (0, z, 0, 0))
            out_shape = jax.ShapeDtypeStruct((local_vel, depth, width_x, width_y), jnp.bfloat16)
        else:
            in_specs.append(pl.BlockSpec((rank, local_vel), lambda z: (0, 0)))
            out_specs = [
                pl.BlockSpec((local_vel, plane), lambda z: (0, z)),
                pl.BlockSpec((rank, plane), lambda z: (0, z)),
            ]
            out_shape = [
                jax.ShapeDtypeStruct((local_vel, cells), jnp.bfloat16),
                jax.ShapeDtypeStruct((rank, cells), jnp.float32),
            ]
        return pl.pallas_call(
            collide_kernel,
            grid=(depth,),
            in_specs=in_specs,
            out_specs=out_specs,
            out_shape=out_shape,
            compiler_params=pltpu.CompilerParams(vmem_limit_bytes=48 * 1024 * 1024),
        )

    current = distribution.reshape(local_vel, cells)
    down_t = down_factor.T
    up_order = jnp.take(up_factor, gather_order(rank), axis=1)
    partial = lax.dot_general(
        down_factor, current, (((0,), (0,)), ((), ())), preferred_element_type=jnp.float32
    )
    for step in range(STEPS):
        low_face = current[:, :plane]
        high_face = current[:, cells - plane:]
        out_low = jnp.sum(wl[:, None] * low_face.astype(jnp.float32), axis=0)
        out_high = jnp.sum(wh[:, None] * high_face.astype(jnp.float32), axis=0)
        outflux = vel_sum(jnp.stack([out_low, out_high]))
        ghost_low = wall_ghost(outflux[0], wall_kind[0].reshape(plane), maxwell, energy, norm)
        ghost_high = wall_ghost(outflux[1], wall_kind[1].reshape(plane), maxwell, energy, norm)
        from_below = lax.ppermute(high_face, "space", forward)
        from_above = lax.ppermute(low_face, "space", backward)
        lower_plane = jnp.where(slab == 0, ghost_low, from_below.astype(jnp.float32))
        upper_plane = jnp.where(slab == slabs - 1, ghost_high, from_above.astype(jnp.float32))
        coeffs = lax.psum_scatter(partial, "vel", scatter_dimension=0, tiled=True)
        base = transport(params, current, lower_plane, upper_plane)
        coeffs, base = lax.optimization_barrier((coeffs, base))
        quarters = gather_rows(coeffs.astype(jnp.bfloat16))
        if step == STEPS - 1:
            current = collide_call(True)(up_order, *quarters, base)
        else:
            current, partial = collide_call(False)(up_order, *quarters, base, down_t)
    return current


def solution(mesh):
    return jax.shard_map(
        body,
        mesh=mesh,
        in_specs=(P("vel", "space", None, None), P("vel", None), P("vel", None), P("vel"), P()),
        out_specs=P("vel", "space", None, None),
        check_vma=False,
    )
```

```python
import functools

import jax
import jax.numpy as jnp
from jax import lax
from jax.experimental import pallas as pl
from jax.experimental.pallas import tpu as pltpu
from jax.sharding import PartitionSpec as P


NV = 16
STEPS = 2


speed_range = 8.0
time_ratio = 0.08
wall_heat = 3.0


def components(vel_ids):
    spacing = speed_range / NV
    midpoint = (NV - 1) / 2.0
    along_z = ((vel_ids // (NV * NV)).astype(jnp.float32) - midpoint) * spacing
    along_x = ((vel_ids // NV % NV).astype(jnp.float32) - midpoint) * spacing
    along_y = ((vel_ids % NV).astype(jnp.float32) - midpoint) * spacing
    return (along_z, along_x, along_y)


def wall_ghost(outflux, kind_face, maxwell, energy, norm):
    sigma = outflux / norm
    heating = jnp.where(kind_face == 1, wall_heat, 0.0)
    opened = jnp.where(kind_face == 2, 0.0, 1.0)
    return (
        maxwell[:, None]
        * (sigma[None] + heating[None] * energy[:, None])
        * opened[None]
    )


def transport_kernel(par_ref, cur_ref, lo_ref, hi_ref, out_ref, work_ref, *, depth, plane, width):
    work_ref[:, 0:plane] = lo_ref[...]
    work_ref[:, (depth + 1) * plane:(depth + 2) * plane] = hi_ref[...]
    work_ref[:, plane:(depth + 1) * plane] = cur_ref[...].astype(jnp.float32)
    rows = plane // width

    def one_plane(z, carry):
        base = pl.multiple_of((z + 1) * plane, plane)
        for x in range(rows):
            at = base + x * width
            xm = base + ((x - 1) % rows) * width
            xp = base + ((x + 1) % rows) * width
            c = work_ref[:, pl.ds(at, width)]
            lo = work_ref[:, pl.ds(at - plane, width)]
            hi = work_ref[:, pl.ds(at + plane, width)]
            left = work_ref[:, pl.ds(xm, width)]
            right = work_ref[:, pl.ds(xp, width)]
            down_y = pltpu.roll(c, 1, 1)
            up_y = pltpu.roll(c, width - 1, 1)
            total = (
                par_ref[0] * c
                + par_ref[1] * lo
                + par_ref[2] * hi
                + par_ref[3] * left
                + par_ref[4] * right
                + par_ref[5] * down_y
                + par_ref[6] * up_y
            )
            out_ref[:, pl.ds(pl.multiple_of(z * plane + x * width, width), width)] = total
        return carry

    lax.fori_loop(0, depth, one_plane, 0)


def collide_kernel(up_ref, coef_ref, coef_far_ref, base_ref, *rest):
    split = coef_ref.shape[0]
    gained = jnp.dot(up_ref[:, :split], coef_ref[...], preferred_element_type=jnp.float32)
    gained = gained + jnp.dot(up_ref[:, split:], coef_far_ref[...], preferred_element_type=jnp.float32)
    total = base_ref[...] + time_ratio * gained
    if len(rest) == 1:
        out_ref = rest[0]
        shape = (out_ref.shape[0], out_ref.shape[2], out_ref.shape[3])
        out_ref[:, 0] = total.reshape(shape).astype(out_ref.dtype)
    else:
        down_t_ref, out_ref, partial_ref = rest
        stored = total.astype(out_ref.dtype)
        out_ref[...] = stored
        partial_ref[...] = jnp.dot(down_t_ref[...], stored, preferred_element_type=jnp.float32)


def swap(value, hop):
    count = lax.axis_size("vel")
    return lax.ppermute(value, "vel", [(i, i ^ hop) for i in range(count)])


def gather_hops():
    count = lax.axis_size("vel")
    levels = count.bit_length() - 1
    return [1 << b for b in range(levels - 1, 0, -1)], [1 << b for b in range(1, levels)]


def gather_rows(shard):
    half = shard.shape[0] // 2
    first, second = shard[:half], shard[half:]
    for hop_a, hop_b in zip(*gather_hops()):
        first = jnp.concatenate([first, swap(first, hop_a)])
        second = jnp.concatenate([second, swap(second, hop_b)])
    value = jnp.concatenate([first, second])
    return value, swap(value, 1)


def gather_order(rank):
    me = lax.axis_index("vel")
    count = lax.axis_size("vel")
    hops_a, hops_b = gather_hops()
    shard = rank // count
    half = shard // 2
    span = len(hops_a)
    place = jnp.arange(rank, dtype=jnp.int32)
    row = place % half
    pos = (place // half) % (1 << span)
    part = (place // (half << span)) % 2
    source = (place // (half << (span + 1))) ^ (me % 2)
    for k in range(span):
        hop = jnp.where(part == 0, hops_a[k], hops_b[k])
        source = source + (((pos >> k) & 1) ^ ((me // hop) % 2)) * hop
    return source * shard + part * half + row


def vel_sum(value):
    count = lax.axis_size("vel")
    hop = 1
    while hop < count:
        value = value + lax.ppermute(value, "vel", [(i, i ^ hop) for i in range(count)])
        hop *= 2
    return value


def body(distribution, up_factor, down_factor, decay, wall_kind):
    local_vel, depth, width_x, width_y = distribution.shape
    plane = width_x * width_y
    cells = depth * plane
    rank = up_factor.shape[1]
    vel_ids = lax.axis_index("vel") * local_vel + jnp.arange(local_vel, dtype=jnp.int32)
    along_z, along_x, along_y = components(vel_ids)
    speed_sq = along_z * along_z + along_x * along_x + along_y * along_y
    maxwell = jnp.exp(-0.5 * speed_sq)
    energy = 0.5 * speed_sq - 1.5
    all_ids = jnp.arange(NV**3, dtype=jnp.int32)
    full_z, full_x, full_y = components(all_ids)
    norm = jnp.sum(
        jnp.maximum(full_z, 0.0)
        * jnp.exp(-0.5 * (full_z * full_z + full_x * full_x + full_y * full_y))
    )
    slab = lax.axis_index("space")
    slabs = lax.axis_size("space")
    dt = time_ratio
    per_vel = jnp.stack(
        [
            1.0 - dt * (jnp.abs(along_z) + jnp.abs(along_x) + jnp.abs(along_y)) - dt * decay,
            dt * jnp.maximum(along_z, 0.0),
            -dt * jnp.minimum(along_z, 0.0),
            dt * jnp.maximum(along_x, 0.0),
            -dt * jnp.minimum(along_x, 0.0),
            dt * jnp.maximum(along_y, 0.0),
            -dt * jnp.minimum(along_y, 0.0),
        ]
    )
    params = jnp.broadcast_to(per_vel[:, :, None], (7, local_vel, width_y))
    wl = jnp.maximum(-along_z, 0.0)
    wh = jnp.maximum(along_z, 0.0)
    count = slabs
    forward = [(i, i + 1) for i in range(count - 1)]
    backward = [(i + 1, i) for i in range(count - 1)]

    vb = 128
    transport = pl.pallas_call(
        functools.partial(transport_kernel, depth=depth, plane=plane, width=width_y),
        grid=(local_vel // vb,),
        in_specs=[
            pl.BlockSpec((7, vb, width_y), lambda i: (0, i, 0)),
            pl.BlockSpec((vb, cells), lambda i: (i, 0)),
            pl.BlockSpec((vb, plane), lambda i: (i, 0)),
            pl.BlockSpec((vb, plane), lambda i: (i, 0)),
        ],
        out_specs=pl.BlockSpec((vb, cells), lambda i: (i, 0)),
        out_shape=jax.ShapeDtypeStruct((local_vel, cells), jnp.float32),
        scratch_shapes=[pltpu.VMEM((vb, cells + 2 * plane), jnp.float32)],
        compiler_params=pltpu.CompilerParams(vmem_limit_bytes=48 * 1024 * 1024),
    )
    def collide_call(final):
        block = plane if final else plane // 2
        in_specs = [
            pl.BlockSpec((local_vel, rank), lambda z: (0, 0)),
            pl.BlockSpec((rank // 2, block), lambda z: (0, z)),
            pl.BlockSpec((rank // 2, block), lambda z: (0, z)),
            pl.BlockSpec((local_vel, block), lambda z: (0, z)),
        ]
        if final:
            out_specs = pl.BlockSpec((local_vel, 1, width_x, width_y), lambda z: (0, z, 0, 0))
            out_shape = jax.ShapeDtypeStruct((local_vel, depth, width_x, width_y), jnp.bfloat16)
        else:
            in_specs.append(pl.BlockSpec((rank, local_vel), lambda z: (0, 0)))
            out_specs = [
                pl.BlockSpec((local_vel, block), lambda z: (0, z)),
                pl.BlockSpec((rank, block), lambda z: (0, z)),
            ]
            out_shape = [
                jax.ShapeDtypeStruct((local_vel, cells), jnp.bfloat16),
                jax.ShapeDtypeStruct((rank, cells), jnp.float32),
            ]
        return pl.pallas_call(
            collide_kernel,
            grid=(cells // block,),
            in_specs=in_specs,
            out_specs=out_specs,
            out_shape=out_shape,
            compiler_params=pltpu.CompilerParams(vmem_limit_bytes=48 * 1024 * 1024),
        )

    current = distribution.reshape(local_vel, cells)
    down_t = down_factor.T
    up_order = jnp.take(up_factor, gather_order(rank), axis=1)
    partial = lax.dot_general(
        down_factor, current, (((0,), (0,)), ((), ())), preferred_element_type=jnp.float32
    )
    for step in range(STEPS):
        low_face = current[:, :plane]
        high_face = current[:, cells - plane:]
        out_low = jnp.sum(wl[:, None] * low_face.astype(jnp.float32), axis=0)
        out_high = jnp.sum(wh[:, None] * high_face.astype(jnp.float32), axis=0)
        outflux = vel_sum(jnp.stack([out_low, out_high]))
        ghost_low = wall_ghost(outflux[0], wall_kind[0].reshape(plane), maxwell, energy, norm)
        ghost_high = wall_ghost(outflux[1], wall_kind[1].reshape(plane), maxwell, energy, norm)
        from_below = lax.ppermute(high_face, "space", forward)
        from_above = lax.ppermute(low_face, "space", backward)
        lower_plane = jnp.where(slab == 0, ghost_low, from_below.astype(jnp.float32))
        upper_plane = jnp.where(slab == slabs - 1, ghost_high, from_above.astype(jnp.float32))
        coeffs = lax.psum_scatter(partial, "vel", scatter_dimension=0, tiled=True)
        base = transport(params, current, lower_plane, upper_plane)
        coeffs, base = lax.optimization_barrier((coeffs, base))
        near, far = gather_rows(coeffs.astype(jnp.bfloat16))
        if step == STEPS - 1:
            current = collide_call(True)(up_order, near, far, base)
        else:
            current, partial = collide_call(False)(up_order, near, far, base, down_t)
    return current


def solution(mesh):
    return jax.shard_map(
        body,
        mesh=mesh,
        in_specs=(P("vel", "space", None, None), P("vel", None), P("vel", None), P("vel"), P()),
        out_specs=P("vel", "space", None, None),
        check_vma=False,
    )
```
